512 devices in a mesh: tm: 128 (over y, x, z_hi, core), stream: 4 (over z_lo).
Axes of the slice: x: 4, y: 8, z: 8 (z_hi: 2, z_lo: 4; z = z_hi * 4 + z_lo), core: 2. Of those that a mesh axis runs over, the one named last changes fastest.
Arguments:
- series: bfloat16 [4, 16384, 1024], P('stream', 'tm')
- loss_grad: bfloat16 [4, 16384, 1024], P('stream', 'tm'), may hold values from -6 to 6
- query_weight: bfloat16 [1024, 1024], P('stream')
- keyval_weight: bfloat16 [1024, 512], P('stream')
- output_weight: bfloat16 [1024, 1024], P('stream'), may hold values from -0.1875 to 0.1875
- lengths: int32 [4], P('stream'), may hold values from 1 to 16384, as said below
Outputs:
- series_grad: bfloat16 [4, 16384, 1024], P('stream', 'tm')
- keyval_grad: float32 [1024, 512], P('stream')
The draws below stay inside these ranges and needn't reach their ends.
Inputs may be any that keep to these rules, and one draw needn't show every extreme that they name: `lengths`: one recording in every draw has all 16384 positions valid.
All inputs are finite; a program needn't handle non-finite values.
Results may differ from the reference program's by a relative error of at most 0.025.
The reference program's roundings to bfloat16 on the way (of `queries`, `keyvals`, `probs`, `attn`, `attn_grad`, `score_grad`, `query_grad` and `keyval_grads`) count: a program that leaves them out, or rounds other values in their place, can miss the bound.
Values may be sent and summed in bfloat16 or wider, within the bound.
No kernel may reach another device: no remote copies, remote signals or barrier semaphores. Data moves between devices by JAX's collectives and lax.ppermute only.
A program may use at most 64 MiB of HBM per device.

```python
import jax
import jax.numpy as jnp
from jax import lax

D = 1024
HEADS = 16
KV_HEADS = 4
HEAD_DIM = 64
TOK_DEV = 128
WINDOW = 512
Q_WIDTH = 1024
KV_WIDTH = 512
LEN = 16384
RECORDS = 4


def shared_query(key):
    return jax.random.normal(jax.random.fold_in(key, 11), (D, Q_WIDTH), jnp.float32) * D ** (-0.5)


def draw_query_weight(key, part):
    return shared_query(key).astype(jnp.bfloat16)


def draw_keyval_weight(key, part):
    fresh_matrix = jax.random.normal(jax.random.fold_in(key, 12), (D, KV_WIDTH), jnp.float32) * D ** (-0.5)
    return fresh_matrix.astype(jnp.bfloat16)


def draw_series(key, part):
    shape_full = (RECORDS, LEN, D)
    base_rows = jax.random.truncated_normal(jax.random.fold_in(key, 21), -6.0, 6.0, shape_full, jnp.float32)
    return base_rows.astype(jnp.bfloat16)


def draw_lengths(key, part):
    drawn = jax.random.randint(jax.random.fold_in(key, 31), (RECORDS,), 1, LEN + 1, jnp.int32)
    full_one = jax.random.randint(jax.random.fold_in(key, 32), (), 0, RECORDS, jnp.int32)
    return jnp.where(jnp.arange(RECORDS, dtype=jnp.int32) == full_one, LEN, drawn).astype(jnp.int32)


def level_of(key, shape, shards, low, top_value):
    gain = 1.0
    for position, parts in shards:
        heights = jax.random.uniform(jax.random.fold_in(jax.random.fold_in(key, 6), position), (parts,), jnp.float32, low / len(shards), top_value / len(shards))
        gain = gain * jnp.repeat(jnp.exp(heights), shape[position] // parts).reshape((-1,) + (1,) * (len(shape) - 1 - position))
    return gain


def noise(stream_key, extent, deviation, bound, split=(), kind=jnp.bfloat16):
    loudness = level_of(stream_key, extent, split, -0.22, 0.18) if split else 1.0
    values = jax.random.normal(stream_key, extent, jnp.float32) * deviation * loudness
    return jnp.minimum(jnp.maximum(values, -bound), bound).astype(kind)


def setup_inputs(seed: int = 0) -> dict:
    streams_of = jax.random.split(jax.random.key(seed), 7)
    return {
        "series": draw_series(jax.random.fold_in(streams_of[6], 71), 0),
        "loss_grad": noise(streams_of[1], (RECORDS, LEN, D), 1.0, 6.0, ((0, 4), (1, 128))),
        "query_weight": draw_query_weight(jax.random.fold_in(streams_of[6], 71), 0),
        "keyval_weight": draw_keyval_weight(jax.random.fold_in(streams_of[6], 71), 0),
        "output_weight": noise(streams_of[4], (Q_WIDTH, D), Q_WIDTH ** -0.5, 0.1875, ((0, 4),)),
        "lengths": draw_lengths(jax.random.fold_in(streams_of[6], 71), 0),
    }


def barrier_round(values):
    return lax.optimization_barrier(values.astype(jnp.bfloat16)).astype(jnp.float32)


def reference(series, loss_grad, query_weight, keyval_weight, output_weight, lengths):
    group_size = HEADS // KV_HEADS
    tile_rows = min(128, TOK_DEV)
    key_span = WINDOW + tile_rows
    score_scale = HEAD_DIM ** -0.5
    key_width = KV_HEADS * HEAD_DIM
    grad_total = jnp.zeros((D, KV_WIDTH), jnp.float32)
    input_grads = []
    for record in range(RECORDS):
        record_rows = series[record]
        outer_grad = loss_grad[record]
        valid_count = lengths[record]
        queries = jnp.dot(record_rows, query_weight, preferred_element_type=jnp.float32).astype(jnp.bfloat16)
        keyvals = jnp.dot(record_rows, keyval_weight, preferred_element_type=jnp.float32).astype(jnp.bfloat16)
        attn_grad = jnp.dot(outer_grad, output_weight.T, preferred_element_type=jnp.float32).astype(jnp.bfloat16)
        padded_kv = jnp.concatenate([jnp.zeros((WINDOW, KV_WIDTH), jnp.bfloat16), keyvals], axis=0)

        def one_block(accumulated, block_index):
            start_row = block_index * tile_rows
            query_tile = lax.dynamic_slice_in_dim(queries, start_row, tile_rows, 0)
            query_tile = query_tile.reshape(tile_rows, KV_HEADS, group_size, HEAD_DIM).astype(jnp.float32)
            window_rows = lax.dynamic_slice_in_dim(padded_kv, start_row, key_span, 0)
            key_block = window_rows[:, :key_width].reshape(key_span, KV_HEADS, HEAD_DIM).astype(jnp.float32)
            value_block = window_rows[:, key_width:].reshape(key_span, KV_HEADS, HEAD_DIM).astype(jnp.float32)
            scores = jnp.einsum('qgjd,kgd->gjqk', query_tile, key_block) * score_scale
            query_pos = start_row + jnp.arange(tile_rows, dtype=jnp.int32)
            key_pos = start_row - WINDOW + jnp.arange(key_span, dtype=jnp.int32)
            live_rows = query_pos < valid_count
            allowed = (key_pos[None, :] <= query_pos[:, None]) & (query_pos[:, None] - key_pos[None, :] < WINDOW)
            allowed = allowed & (key_pos[None, :] >= 0) & (key_pos[None, :] < valid_count) & live_rows[:, None]
            masked = jnp.where(allowed, scores, -1e30)
            row_max = jnp.max(masked, axis=-1, keepdims=True)
            terms = jnp.where(allowed, jnp.exp(masked - row_max), 0.0)
            denom = jnp.sum(terms, axis=-1, keepdims=True)
            denom = jnp.where(live_rows[:, None], denom, 1.0)
            probs = barrier_round(terms / denom)
            attn = barrier_round(jnp.einsum('gjqk,kgd->qgjd', probs, value_block))
            grad_tile = lax.dynamic_slice_in_dim(attn_grad, start_row, tile_rows, 0)
            grad_tile = grad_tile.reshape(tile_rows, KV_HEADS, group_size, HEAD_DIM).astype(jnp.float32)
            delta = jnp.transpose(jnp.sum(grad_tile * attn, axis=-1), (1, 2, 0))[..., None]
            prob_grad = jnp.einsum('qgjd,kgd->gjqk', grad_tile, value_block)
            score_grad = barrier_round(probs * (prob_grad - delta) * score_scale)
            query_grad = jnp.einsum('gjqk,kgd->qgjd', score_grad, key_block).astype(jnp.bfloat16)
            key_grad = jnp.einsum('gjqk,qgjd->kgd', score_grad, query_tile).reshape(key_span, key_width)
            value_grad = jnp.einsum('gjqk,qgjd->kgd', probs, grad_tile).reshape(key_span, key_width)
            current = lax.dynamic_slice_in_dim(accumulated, start_row, key_span, 0)
            updated = current + jnp.concatenate([key_grad, value_grad], axis=1)
            accumulated = lax.dynamic_update_slice_in_dim(accumulated, updated, start_row, 0)
            return accumulated, query_grad.reshape(tile_rows, Q_WIDTH)

        initial = jnp.zeros((WINDOW + LEN, KV_WIDTH), jnp.float32)
        accumulated, query_blocks = lax.scan(one_block, initial, jnp.arange(LEN // tile_rows, dtype=jnp.int32))
        query_grads = query_blocks.reshape(LEN, Q_WIDTH)
        keyval_grads = accumulated[WINDOW:].astype(jnp.bfloat16)
        series_part = jnp.dot(query_grads, query_weight.T, preferred_element_type=jnp.float32)
        series_part = series_part + jnp.dot(keyval_grads, keyval_weight.T, preferred_element_type=jnp.float32)
        input_grads.append(series_part.astype(jnp.bfloat16))
        grad_total = grad_total + jnp.dot(record_rows.T, keyval_grads, preferred_element_type=jnp.float32)
    return jnp.stack(input_grads), grad_total
```

```python
import jax
import jax.numpy as jnp
from jax import lax
from jax.sharding import PartitionSpec as P

HEADS = 16
KV_HEADS = 4
HEAD_DIM = 64
REACH = 4


def shifted(value, axis, steps):
    count = lax.axis_size(axis)
    leading, last = (max(0, -steps), min(count, count - steps))
    return lax.ppermute(value, axis, [(source, source + steps) for source in range(leading, last)])


def xor_swap(value, axis, bit):
    count = lax.axis_size(axis)
    return lax.ppermute(value, axis, [(source, source ^ (1 << bit)) for source in range(count)])


def tree_psum(value, axis):
    count = lax.axis_size(axis)
    bits = count.bit_length() - 1
    if count != 1 << bits or value.shape[0] % count:
        return lax.psum(value, axis)
    order = [b for b in (0, 2, 4, 1, 3, 5, 6) if b < bits] + list(range(7, bits))
    index = lax.axis_index(axis)
    current = value
    for bit in order:
        half = current.shape[0] // 2
        upper = ((index >> bit) & 1) == 1
        low, high = current[:half], current[half:]
        keep = jnp.where(upper, high, low)
        send = jnp.where(upper, low, high)
        current = keep + xor_swap(send, axis, bit)
    for bit in reversed(order):
        upper = ((index >> bit) & 1) == 1
        other = xor_swap(current, axis, bit)
        current = jnp.where(
            upper, jnp.concatenate([other, current]), jnp.concatenate([current, other])
        )
    return current


def contract_last(left, right):
    return lax.dot_general(
        left, right, (((1,), (1,)), ((), ())), preferred_element_type=jnp.float32
    )


def contract_first(left, right):
    return lax.dot_general(
        left, right, (((0,), (0,)), ((), ())), preferred_element_type=jnp.float32
    )


def per_device(series, loss_grad, query_weight, keyval_weight, output_weight, lengths):
    record_rows = series[0]
    outer_grad = loss_grad[0]
    valid_count = lengths[0]
    shard_tokens = record_rows.shape[0]
    keyval_width = keyval_weight.shape[1]
    key_width = keyval_width // 2
    group_size = HEADS // KV_HEADS
    tile_rows = min(128, shard_tokens)
    key_span = REACH * shard_tokens + tile_rows
    score_scale = HEAD_DIM ** (-0.5)
    anchor = lax.axis_index("tm") * shard_tokens
    query_full, keyval_full = (
        lax.all_gather(query_weight, "stream", axis=0, tiled=True),
        lax.all_gather(keyval_weight, "stream", axis=0, tiled=True),
    )
    queries = jnp.dot(record_rows, query_full, preferred_element_type=jnp.float32).astype(
        jnp.bfloat16
    )
    keyvals = jnp.dot(record_rows, keyval_full, preferred_element_type=jnp.float32).astype(
        jnp.bfloat16
    )
    attn_grad = contract_last(
        outer_grad, lax.all_gather(output_weight, "stream", axis=0, tiled=True)
    ).astype(jnp.bfloat16)
    earlier = [shifted(keyvals, "tm", offset) for offset in range(REACH, 0, -1)]
    window_keyvals = jnp.concatenate(earlier + [keyvals], axis=0)
    key_parts = []
    value_parts = []
    query_grads = []
    for head_group in range(KV_HEADS):
        query_cols = slice(
            head_group * group_size * HEAD_DIM, (head_group + 1) * group_size * HEAD_DIM
        )
        key_cols = slice(head_group * HEAD_DIM, (head_group + 1) * HEAD_DIM)
        value_cols = slice(
            key_width + head_group * HEAD_DIM, key_width + (head_group + 1) * HEAD_DIM
        )
        group_key = None
        group_value = None
        query_tile = queries[0:tile_rows, query_cols].reshape(tile_rows, group_size, HEAD_DIM)
        key_tile = window_keyvals[0:key_span, key_cols]
        value_tile = window_keyvals[0:key_span, value_cols]
        query_pos = anchor + 0 + jnp.arange(tile_rows, dtype=jnp.int32)
        key_pos = anchor - REACH * shard_tokens + 0 + jnp.arange(key_span, dtype=jnp.int32)
        live_rows = query_pos < valid_count
        allowed = (key_pos[None, :] <= query_pos[:, None]) & (
            query_pos[:, None] - key_pos[None, :] < REACH * shard_tokens
        )
        allowed = (
            allowed
            & (key_pos[None, :] >= 0)
            & (key_pos[None, :] < valid_count)
            & live_rows[:, None]
        )
        scores = (
            jnp.einsum("qjd,kd->jqk", query_tile, key_tile, preferred_element_type=jnp.float32)
            * score_scale
        )
        masked = jnp.where(allowed, scores, -1e30)
        row_max = jnp.max(masked, axis=-1, keepdims=True)
        terms = jnp.where(allowed, jnp.exp(masked - row_max), 0.0)
        denom = jnp.sum(terms, axis=-1, keepdims=True)
        denom = jnp.where(live_rows[:, None], denom, 1.0)
        attn_probs = (terms / denom).astype(jnp.bfloat16)
        attn_tile = jnp.einsum(
            "jqk,kd->qjd", attn_probs, value_tile, preferred_element_type=jnp.float32
        ).astype(jnp.bfloat16)
        grad_tile = attn_grad[0:tile_rows, query_cols].reshape(tile_rows, group_size, HEAD_DIM)
        row_delta = jnp.sum(
            grad_tile.astype(jnp.float32) * attn_tile.astype(jnp.float32), axis=-1
        ).T[:, :, None]
        prob_grad = jnp.einsum(
            "qjd,kd->jqk", grad_tile, value_tile, preferred_element_type=jnp.float32
        )
        score_grad = (
            attn_probs.astype(jnp.float32) * (prob_grad - row_delta) * score_scale
        ).astype(jnp.bfloat16)
        query_grad = jnp.einsum(
            "jqk,kd->qjd", score_grad, key_tile, preferred_element_type=jnp.float32
        ).astype(jnp.bfloat16)
        key_grad = jnp.einsum(
            "jqk,qjd->kd", score_grad, query_tile, preferred_element_type=jnp.float32
        )
        value_grad = jnp.einsum(
            "jqk,qjd->kd", attn_probs, grad_tile, preferred_element_type=jnp.float32
        )
        group_key = key_grad
        group_value = value_grad
        tile_list = query_grad.reshape(tile_rows, group_size * HEAD_DIM)
        key_parts.append(group_key)
        value_parts.append(group_value)
        query_grads.append(tile_list)
    query_grad_all = jnp.concatenate(query_grads, axis=1)
    partial_value = jnp.concatenate(key_parts + value_parts, axis=1)

    def shard_slot(offset):
        return partial_value[(REACH - offset) * shard_tokens : (REACH - offset + 1) * shard_tokens]

    summed = shard_slot(0)
    for offset in range(1, REACH + 1):
        summed = summed + shifted(shard_slot(offset).astype(jnp.bfloat16), "tm", -offset).astype(
            jnp.float32
        )
    keyval_grads = summed.astype(jnp.bfloat16)
    input_grad = contract_last(query_grad_all, query_full) + contract_last(
        keyval_grads, keyval_full
    )
    input_grad = input_grad.astype(jnp.bfloat16)
    grad_shard = lax.psum_scatter(
        contract_first(record_rows, keyval_grads).astype(jnp.bfloat16),
        "stream",
        scatter_dimension=0,
        tiled=True,
    ).astype(jnp.float32)
    weight_grad = tree_psum(grad_shard, "tm")
    return (input_grad[None], weight_grad)


def solution(mesh):
    placed = (
        P("stream", "tm", None),
        P("stream", "tm", None),
        P("stream", None),
        P("stream", None),
        P("stream", None),
        P("stream"),
    )
    return jax.shard_map(
        per_device,
        mesh=mesh,
        in_specs=placed,
        out_specs=(P("stream", "tm", None), P("stream", None)),
        check_vma=False,
    )
```

```python
import jax
import jax.numpy as jnp
from jax import lax
from jax.sharding import PartitionSpec as P

HEADS = 16
KV_HEADS = 4
HEAD_DIM = 64
REACH = 4


def shifted(value, axis, steps):
    count = lax.axis_size(axis)
    leading, last = (max(0, -steps), min(count, count - steps))
    return lax.ppermute(value, axis, [(source, source + steps) for source in range(leading, last)])


def xor_swap(value, axis, bit):
    count = lax.axis_size(axis)
    return lax.ppermute(value, axis, [(source, source ^ (1 << bit)) for source in range(count)])


def tree_psum(value, axis):
    count = lax.axis_size(axis)
    bits = count.bit_length() - 1
    if count != 1 << bits or value.shape[0] % count:
        return lax.psum(value, axis)
    order = [b for b in (0, 2, 4, 1, 3, 5, 6) if b < bits] + list(range(7, bits))
    index = lax.axis_index(axis)
    current = value
    for bit in order:
        half = current.shape[0] // 2
        upper = ((index >> bit) & 1) == 1
        low, high = current[:half], current[half:]
        keep = jnp.where(upper, high, low)
        send = jnp.where(upper, low, high)
        current = keep + xor_swap(send, axis, bit)
    for bit in reversed(order):
        upper = ((index >> bit) & 1) == 1
        other = xor_swap(current, axis, bit)
        current = jnp.where(
            upper, jnp.concatenate([other, current]), jnp.concatenate([current, other])
        )
    return current


def contract_last(left, right):
    return lax.dot_general(
        left, right, (((1,), (1,)), ((), ())), preferred_element_type=jnp.float32
    )


def contract_first(left, right):
    return lax.dot_general(
        left, right, (((0,), (0,)), ((), ())), preferred_element_type=jnp.float32
    )


def per_device(series, loss_grad, query_weight, keyval_weight, output_weight, lengths):
    record_rows = series[0]
    outer_grad = loss_grad[0]
    valid_count = lengths[0]
    shard_tokens = record_rows.shape[0]
    keyval_width = keyval_weight.shape[1]
    key_width = keyval_width // 2
    group_size = HEADS // KV_HEADS
    tile_rows = min(128, shard_tokens)
    key_span = REACH * shard_tokens + tile_rows
    score_scale = HEAD_DIM ** (-0.5)
    anchor = lax.axis_index("tm") * shard_tokens
    query_width = query_weight.shape[1]
    weights_full = lax.all_gather(
        jnp.concatenate([query_weight, keyval_weight, output_weight], axis=1),
        "stream",
        axis=0,
        tiled=True,
    )
    query_full = weights_full[:, :query_width]
    keyval_full = weights_full[:, query_width : query_width + keyval_width]
    output_full = weights_full[:, query_width + keyval_width :]
    queries = jnp.dot(record_rows, query_full, preferred_element_type=jnp.float32).astype(
        jnp.bfloat16
    )
    keyvals = jnp.dot(record_rows, keyval_full, preferred_element_type=jnp.float32).astype(
        jnp.bfloat16
    )
    attn_grad = contract_last(outer_grad, output_full).astype(jnp.bfloat16)
    earlier = [shifted(keyvals, "tm", offset) for offset in range(REACH, 0, -1)]
    window_keyvals = jnp.concatenate(earlier + [keyvals], axis=0)
    key_parts = []
    value_parts = []
    query_grads = []
    for head_group in range(KV_HEADS):
        query_cols = slice(
            head_group * group_size * HEAD_DIM, (head_group + 1) * group_size * HEAD_DIM
        )
        key_cols = slice(head_group * HEAD_DIM, (head_group + 1) * HEAD_DIM)
        value_cols = slice(
            key_width + head_group * HEAD_DIM, key_width + (head_group + 1) * HEAD_DIM
        )
        group_key = None
        group_value = None
        query_tile = queries[0:tile_rows, query_cols].reshape(tile_rows, group_size, HEAD_DIM)
        key_tile = window_keyvals[0:key_span, key_cols]
        value_tile = window_keyvals[0:key_span, value_cols]
        query_pos = anchor + 0 + jnp.arange(tile_rows, dtype=jnp.int32)
        key_pos = anchor - REACH * shard_tokens + 0 + jnp.arange(key_span, dtype=jnp.int32)
        live_rows = query_pos < valid_count
        allowed = (key_pos[None, :] <= query_pos[:, None]) & (
            query_pos[:, None] - key_pos[None, :] < REACH * shard_tokens
        )
        allowed = (
            allowed
            & (key_pos[None, :] >= 0)
            & (key_pos[None, :] < valid_count)
            & live_rows[:, None]
        )
        scores = (
            jnp.einsum("qjd,kd->jqk", query_tile, key_tile, preferred_element_type=jnp.float32)
            * score_scale
        )
        masked = jnp.where(allowed, scores, -1e30)
        row_max = jnp.max(masked, axis=-1, keepdims=True)
        terms = jnp.where(allowed, jnp.exp(masked - row_max), 0.0)
        denom = jnp.sum(terms, axis=-1, keepdims=True)
        denom = jnp.where(live_rows[:, None], denom, 1.0)
        attn_probs = (terms / denom).astype(jnp.bfloat16)
        attn_tile = jnp.einsum(
            "jqk,kd->qjd", attn_probs, value_tile, preferred_element_type=jnp.float32
        ).astype(jnp.bfloat16)
        grad_tile = attn_grad[0:tile_rows, query_cols].reshape(tile_rows, group_size, HEAD_DIM)
        row_delta = jnp.sum(
            grad_tile.astype(jnp.float32) * attn_tile.astype(jnp.float32), axis=-1
        ).T[:, :, None]
        prob_grad = jnp.einsum(
            "qjd,kd->jqk", grad_tile, value_tile, preferred_element_type=jnp.float32
        )
        score_grad = (
            attn_probs.astype(jnp.float32) * (prob_grad - row_delta) * score_scale
        ).astype(jnp.bfloat16)
        query_grad = jnp.einsum(
            "jqk,kd->qjd", score_grad, key_tile, preferred_element_type=jnp.float32
        ).astype(jnp.bfloat16)
        key_grad = jnp.einsum(
            "jqk,qjd->kd", score_grad, query_tile, preferred_element_type=jnp.float32
        )
        value_grad = jnp.einsum(
            "jqk,qjd->kd", attn_probs, grad_tile, preferred_element_type=jnp.float32
        )
        group_key = key_grad
        group_value = value_grad
        tile_list = query_grad.reshape(tile_rows, group_size * HEAD_DIM)
        key_parts.append(group_key)
        value_parts.append(group_value)
        query_grads.append(tile_list)
    query_grad_all = jnp.concatenate(query_grads, axis=1)
    partial_value = jnp.concatenate(key_parts + value_parts, axis=1)

    def shard_slot(offset):
        return partial_value[(REACH - offset) * shard_tokens : (REACH - offset + 1) * shard_tokens]

    summed = shard_slot(0)
    for offset in range(1, REACH + 1):
        summed = summed + shifted(shard_slot(offset).astype(jnp.bfloat16), "tm", -offset).astype(
            jnp.float32
        )
    keyval_grads = summed.astype(jnp.bfloat16)
    input_grad = contract_last(query_grad_all, query_full) + contract_last(
        keyval_grads, keyval_full
    )
    input_grad = input_grad.astype(jnp.bfloat16)
    grad_shard = lax.psum_scatter(
        contract_first(record_rows, keyval_grads).astype(jnp.bfloat16),
        "stream",
        scatter_dimension=0,
        tiled=True,
    ).astype(jnp.float32)
    weight_grad = tree_psum(grad_shard, "tm")
    return (input_grad[None], weight_grad)


def solution(mesh):
    placed = (
        P("stream", "tm", None),
        P("stream", "tm", None),
        P("stream", None),
        P("stream", None),
        P("stream", None),
        P("stream"),
    )
    return jax.shard_map(
        per_device,
        mesh=mesh,
        in_specs=placed,
        out_specs=(P("stream", "tm", None), P("stream", None)),
        check_vma=False,
    )
```

```python
import jax
import jax.numpy as jnp
from jax import lax
from jax.sharding import PartitionSpec as P

HEADS = 16
KV_HEADS = 4
HEAD_DIM = 64
REACH = 4


def shifted(value, axis, steps):
    count = lax.axis_size(axis)
    leading, last = (max(0, -steps), min(count, count - steps))
    return lax.ppermute(value, axis, [(source, source + steps) for source in range(leading, last)])


def xor_swap(value, axis, bit):
    count = lax.axis_size(axis)
    return lax.ppermute(value, axis, [(source, source ^ (1 << bit)) for source in range(count)])


def tree_psum(value, axis):
    count = lax.axis_size(axis)
    bits = count.bit_length() - 1
    if count != 1 << bits or value.shape[0] % count:
        return lax.psum(value, axis)
    order = [b for b in (0, 2, 4, 1, 3, 5, 6) if b < bits] + list(range(7, bits))
    index = lax.axis_index(axis)
    current = value
    for bit in order:
        half = current.shape[0] // 2
        upper = ((index >> bit) & 1) == 1
        low, high = current[:half], current[half:]
        keep = jnp.where(upper, high, low)
        send = jnp.where(upper, low, high)
        current = keep + xor_swap(send, axis, bit)
    for bit in reversed(order):
        upper = ((index >> bit) & 1) == 1
        other = xor_swap(current, axis, bit)
        current = jnp.where(
            upper, jnp.concatenate([other, current]), jnp.concatenate([current, other])
        )
    return current


def digit_target(source, stride, size, offset):
    digit = (source // stride) % size
    return source + (((digit + offset) % size) - digit) * stride


def scatter_stage(value, axis, stride, size, wire):
    block = value.shape[0] // size
    digit = (lax.axis_index(axis) // stride) % size
    count = lax.axis_size(axis)
    total = lax.dynamic_slice_in_dim(value, digit * block, block, 0).astype(jnp.float32)
    for offset in range(1, size):
        part = lax.dynamic_slice_in_dim(value, ((digit + offset) % size) * block, block, 0)
        pairs = [(source, digit_target(source, stride, size, offset)) for source in range(count)]
        total = total + lax.ppermute(part.astype(wire), axis, pairs).astype(jnp.float32)
    return total


def gather_stage(value, axis, stride, size):
    block = value.shape[0]
    digit = (lax.axis_index(axis) // stride) % size
    count = lax.axis_size(axis)
    full = jnp.zeros((block * size,) + value.shape[1:], value.dtype)
    full = lax.dynamic_update_slice_in_dim(full, value, digit * block, 0)
    for offset in range(1, size):
        pairs = [(source, digit_target(source, stride, size, offset)) for source in range(count)]
        moved = lax.ppermute(value, axis, pairs)
        full = lax.dynamic_update_slice_in_dim(full, moved, ((digit - offset) % size) * block, 0)
    return full


TM_STAGES = ((4, 4), (16, 8), (1, 4))


def staged_grad_sum(partial):
    stream_count = lax.axis_size("stream")
    tm_count = lax.axis_size("tm")
    product = 1
    for _, size in TM_STAGES:
        product *= size
    if product != tm_count or partial.shape[0] % (stream_count * tm_count):
        shard = lax.psum_scatter(
            partial.astype(jnp.bfloat16), "stream", scatter_dimension=0, tiled=True
        ).astype(jnp.float32)
        return tree_psum(shard, "tm")
    current = scatter_stage(partial, "stream", 1, stream_count, jnp.bfloat16)
    for stride, size in TM_STAGES:
        current = scatter_stage(current, "tm", stride, size, jnp.float32)
    for stride, size in reversed(TM_STAGES):
        current = gather_stage(current, "tm", stride, size)
    return current


def contract_last(left, right):
    return lax.dot_general(
        left, right, (((1,), (1,)), ((), ())), preferred_element_type=jnp.float32
    )


def contract_first(left, right):
    return lax.dot_general(
        left, right, (((0,), (0,)), ((), ())), preferred_element_type=jnp.float32
    )


def per_device(series, loss_grad, query_weight, keyval_weight, output_weight, lengths):
    record_rows = series[0]
    outer_grad = loss_grad[0]
    valid_count = lengths[0]
    shard_tokens = record_rows.shape[0]
    keyval_width = keyval_weight.shape[1]
    key_width = keyval_width // 2
    group_size = HEADS // KV_HEADS
    tile_rows = min(128, shard_tokens)
    key_span = REACH * shard_tokens + tile_rows
    score_scale = HEAD_DIM ** (-0.5)
    anchor = lax.axis_index("tm") * shard_tokens
    query_width = query_weight.shape[1]
    weights_full = lax.all_gather(
        jnp.concatenate([query_weight, keyval_weight, output_weight], axis=1),
        "stream",
        axis=0,
        tiled=True,
    )
    query_full = weights_full[:, :query_width]
    keyval_full = weights_full[:, query_width : query_width + keyval_width]
    output_full = weights_full[:, query_width + keyval_width :]
    queries = jnp.dot(record_rows, query_full, preferred_element_type=jnp.float32).astype(
        jnp.bfloat16
    )
    keyvals = jnp.dot(record_rows, keyval_full, preferred_element_type=jnp.float32).astype(
        jnp.bfloat16
    )
    attn_grad = contract_last(outer_grad, output_full).astype(jnp.bfloat16)
    earlier = [shifted(keyvals, "tm", offset) for offset in range(REACH, 0, -1)]
    window_keyvals = jnp.concatenate(earlier + [keyvals], axis=0)
    key_parts = []
    value_parts = []
    query_grads = []
    for head_group in range(KV_HEADS):
        query_cols = slice(
            head_group * group_size * HEAD_DIM, (head_group + 1) * group_size * HEAD_DIM
        )
        key_cols = slice(head_group * HEAD_DIM, (head_group + 1) * HEAD_DIM)
        value_cols = slice(
            key_width + head_group * HEAD_DIM, key_width + (head_group + 1) * HEAD_DIM
        )
        group_key = None
        group_value = None
        query_tile = queries[0:tile_rows, query_cols].reshape(tile_rows, group_size, HEAD_DIM)
        key_tile = window_keyvals[0:key_span, key_cols]
        value_tile = window_keyvals[0:key_span, value_cols]
        query_pos = anchor + 0 + jnp.arange(tile_rows, dtype=jnp.int32)
        key_pos = anchor - REACH * shard_tokens + 0 + jnp.arange(key_span, dtype=jnp.int32)
        live_rows = query_pos < valid_count
        allowed = (key_pos[None, :] <= query_pos[:, None]) & (
            query_pos[:, None] - key_pos[None, :] < REACH * shard_tokens
        )
        allowed = (
            allowed
            & (key_pos[None, :] >= 0)
            & (key_pos[None, :] < valid_count)
            & live_rows[:, None]
        )
        scores = (
            jnp.einsum("qjd,kd->jqk", query_tile, key_tile, preferred_element_type=jnp.float32)
            * score_scale
        )
        masked = jnp.where(allowed, scores, -1e30)
        row_max = jnp.max(masked, axis=-1, keepdims=True)
        terms = jnp.where(allowed, jnp.exp(masked - row_max), 0.0)
        denom = jnp.sum(terms, axis=-1, keepdims=True)
        denom = jnp.where(live_rows[:, None], denom, 1.0)
        attn_probs = (terms / denom).astype(jnp.bfloat16)
        attn_tile = jnp.einsum(
            "jqk,kd->qjd", attn_probs, value_tile, preferred_element_type=jnp.float32
        ).astype(jnp.bfloat16)
        grad_tile = attn_grad[0:tile_rows, query_cols].reshape(tile_rows, group_size, HEAD_DIM)
        row_delta = jnp.sum(
            grad_tile.astype(jnp.float32) * attn_tile.astype(jnp.float32), axis=-1
        ).T[:, :, None]
        prob_grad = jnp.einsum(
            "qjd,kd->jqk", grad_tile, value_tile, preferred_element_type=jnp.float32
        )
        score_grad = (
            attn_probs.astype(jnp.float32) * (prob_grad - row_delta) * score_scale
        ).astype(jnp.bfloat16)
        query_grad = jnp.einsum(
            "jqk,kd->qjd", score_grad, key_tile, preferred_element_type=jnp.float32
        ).astype(jnp.bfloat16)
        key_grad = jnp.einsum(
            "jqk,qjd->kd", score_grad, query_tile, preferred_element_type=jnp.float32
        )
        value_grad = jnp.einsum(
            "jqk,qjd->kd", attn_probs, grad_tile, preferred_element_type=jnp.float32
        )
        group_key = key_grad
        group_value = value_grad
        tile_list = query_grad.reshape(tile_rows, group_size * HEAD_DIM)
        key_parts.append(group_key)
        value_parts.append(group_value)
        query_grads.append(tile_list)
    query_grad_all = jnp.concatenate(query_grads, axis=1)
    partial_value = jnp.concatenate(key_parts + value_parts, axis=1)

    def shard_slot(offset):
        return partial_value[(REACH - offset) * shard_tokens : (REACH - offset + 1) * shard_tokens]

    summed = shard_slot(0)
    for offset in range(1, REACH + 1):
        summed = summed + shifted(shard_slot(offset).astype(jnp.bfloat16), "tm", -offset).astype(
            jnp.float32
        )
    keyval_grads = summed.astype(jnp.bfloat16)
    input_grad = contract_last(query_grad_all, query_full) + contract_last(
        keyval_grads, keyval_full
    )
    input_grad = input_grad.astype(jnp.bfloat16)
    weight_grad = staged_grad_sum(contract_first(record_rows, keyval_grads))
    return (input_grad[None], weight_grad)


def solution(mesh):
    placed = (
        P("stream", "tm", None),
        P("stream", "tm", None),
        P("stream", None),
        P("stream", None),
        P("stream", None),
        P("stream"),
    )
    return jax.shard_map(
        per_device,
        mesh=mesh,
        in_specs=placed,
        out_specs=(P("stream", "tm", None), P("stream", None)),
        check_vma=False,
    )
```

```python
import jax
import jax.numpy as jnp
from jax import lax
from jax.sharding import PartitionSpec as P

HEADS = 16
KV_HEADS = 4
HEAD_DIM = 64
REACH = 4


def shifted(value, axis, steps):
    count = lax.axis_size(axis)
    leading, last = (max(0, -steps), min(count, count - steps))
    return lax.ppermute(value, axis, [(source, source + steps) for source in range(leading, last)])


def xor_swap(value, axis, bit):
    count = lax.axis_size(axis)
    return lax.ppermute(value, axis, [(source, source ^ (1 << bit)) for source in range(count)])


def tree_psum(value, axis):
    count = lax.axis_size(axis)
    bits = count.bit_length() - 1
    if count != 1 << bits or value.shape[0] % count:
        return lax.psum(value, axis)
    order = [b for b in (0, 2, 4, 1, 3, 5, 6) if b < bits] + list(range(7, bits))
    index = lax.axis_index(axis)
    current = value
    for bit in order:
        half = current.shape[0] // 2
        upper = ((index >> bit) & 1) == 1
        low, high = current[:half], current[half:]
        keep = jnp.where(upper, high, low)
        send = jnp.where(upper, low, high)
        current = keep + xor_swap(send, axis, bit)
    for bit in reversed(order):
        upper = ((index >> bit) & 1) == 1
        other = xor_swap(current, axis, bit)
        current = jnp.where(
            upper, jnp.concatenate([other, current]), jnp.concatenate([current, other])
        )
    return current


def halve_stage(value, axis, bit, wire):
    half = value.shape[0] // 2
    upper = ((lax.axis_index(axis) >> bit) & 1) == 1
    low, high = value[:half], value[half:]
    keep = jnp.where(upper, high, low).astype(jnp.float32)
    send = jnp.where(upper, low, high)
    return keep + xor_swap(send.astype(wire), axis, bit).astype(jnp.float32)


def double_stage(value, axis, bit):
    upper = ((lax.axis_index(axis) >> bit) & 1) == 1
    other = xor_swap(value, axis, bit)
    return jnp.where(upper, jnp.concatenate([other, value]), jnp.concatenate([value, other]))


def grad_sum(partial):
    stream_count = lax.axis_size("stream")
    tm_count = lax.axis_size("tm")
    stream_bits = stream_count.bit_length() - 1
    tm_bits = tm_count.bit_length() - 1
    if (
        stream_count != 1 << stream_bits
        or tm_count != 1 << tm_bits
        or partial.shape[0] % (2 * stream_count)
    ):
        shard = lax.psum_scatter(
            partial.astype(jnp.bfloat16), "stream", scatter_dimension=0, tiled=True
        ).astype(jnp.float32)
        return lax.psum(shard, "tm")
    current = partial
    for bit in reversed(range(stream_bits)):
        current = halve_stage(current, "stream", bit, jnp.bfloat16)
    if tm_bits == 0:
        return current
    current = halve_stage(current, "tm", 0, jnp.float32)
    for bit in (2, 4, 1, 3, 5, 6) + tuple(range(7, tm_bits)):
        if bit < tm_bits:
            current = current + xor_swap(current, "tm", bit)
    return double_stage(current, "tm", 0)


def contract_last(left, right):
    return lax.dot_general(
        left, right, (((1,), (1,)), ((), ())), preferred_element_type=jnp.float32
    )


def contract_first(left, right):
    return lax.dot_general(
        left, right, (((0,), (0,)), ((), ())), preferred_element_type=jnp.float32
    )


def per_device(series, loss_grad, query_weight, keyval_weight, output_weight, lengths):
    record_rows = series[0]
    outer_grad = loss_grad[0]
    valid_count = lengths[0]
    shard_tokens = record_rows.shape[0]
    keyval_width = keyval_weight.shape[1]
    key_width = keyval_width // 2
    group_size = HEADS // KV_HEADS
    tile_rows = min(128, shard_tokens)
    key_span = REACH * shard_tokens + tile_rows
    score_scale = HEAD_DIM ** (-0.5)
    anchor = lax.axis_index("tm") * shard_tokens
    query_width = query_weight.shape[1]
    weights_full = lax.all_gather(
        jnp.concatenate([query_weight, keyval_weight, output_weight], axis=1),
        "stream",
        axis=0,
        tiled=True,
    )
    query_full = weights_full[:, :query_width]
    keyval_full = weights_full[:, query_width : query_width + keyval_width]
    output_full = weights_full[:, query_width + keyval_width :]
    queries = jnp.dot(record_rows, query_full, preferred_element_type=jnp.float32).astype(
        jnp.bfloat16
    )
    keyvals = jnp.dot(record_rows, keyval_full, preferred_element_type=jnp.float32).astype(
        jnp.bfloat16
    )
    attn_grad = contract_last(outer_grad, output_full).astype(jnp.bfloat16)
    earlier = [shifted(keyvals, "tm", offset) for offset in range(REACH, 0, -1)]
    window_keyvals = jnp.concatenate(earlier + [keyvals], axis=0)
    key_parts = []
    value_parts = []
    query_grads = []
    for head_group in range(KV_HEADS):
        query_cols = slice(
            head_group * group_size * HEAD_DIM, (head_group + 1) * group_size * HEAD_DIM
        )
        key_cols = slice(head_group * HEAD_DIM, (head_group + 1) * HEAD_DIM)
        value_cols = slice(
            key_width + head_group * HEAD_DIM, key_width + (head_group + 1) * HEAD_DIM
        )
        group_key = None
        group_value = None
        query_tile = queries[0:tile_rows, query_cols].reshape(tile_rows, group_size, HEAD_DIM)
        key_tile = window_keyvals[0:key_span, key_cols]
        value_tile = window_keyvals[0:key_span, value_cols]
        query_pos = anchor + 0 + jnp.arange(tile_rows, dtype=jnp.int32)
        key_pos = anchor - REACH * shard_tokens + 0 + jnp.arange(key_span, dtype=jnp.int32)
        live_rows = query_pos < valid_count
        allowed = (key_pos[None, :] <= query_pos[:, None]) & (
            query_pos[:, None] - key_pos[None, :] < REACH * shard_tokens
        )
        allowed = (
            allowed
            & (key_pos[None, :] >= 0)
            & (key_pos[None, :] < valid_count)
            & live_rows[:, None]
        )
        scores = (
            jnp.einsum("qjd,kd->jqk", query_tile, key_tile, preferred_element_type=jnp.float32)
            * score_scale
        )
        masked = jnp.where(allowed, scores, -1e30)
        row_max = jnp.max(masked, axis=-1, keepdims=True)
        terms = jnp.where(allowed, jnp.exp(masked - row_max), 0.0)
        denom = jnp.sum(terms, axis=-1, keepdims=True)
        denom = jnp.where(live_rows[:, None], denom, 1.0)
        attn_probs = (terms / denom).astype(jnp.bfloat16)
        attn_tile = jnp.einsum(
            "jqk,kd->qjd", attn_probs, value_tile, preferred_element_type=jnp.float32
        ).astype(jnp.bfloat16)
        grad_tile = attn_grad[0:tile_rows, query_cols].reshape(tile_rows, group_size, HEAD_DIM)
        row_delta = jnp.sum(
            grad_tile.astype(jnp.float32) * attn_tile.astype(jnp.float32), axis=-1
        ).T[:, :, None]
        prob_grad = jnp.einsum(
            "qjd,kd->jqk", grad_tile, value_tile, preferred_element_type=jnp.float32
        )
        score_grad = (
            attn_probs.astype(jnp.float32) * (prob_grad - row_delta) * score_scale
        ).astype(jnp.bfloat16)
        query_grad = jnp.einsum(
            "jqk,kd->qjd", score_grad, key_tile, preferred_element_type=jnp.float32
        ).astype(jnp.bfloat16)
        key_grad = jnp.einsum(
            "jqk,qjd->kd", score_grad, query_tile, preferred_element_type=jnp.float32
        )
        value_grad = jnp.einsum(
            "jqk,qjd->kd", attn_probs, grad_tile, preferred_element_type=jnp.float32
        )
        group_key = key_grad
        group_value = value_grad
        tile_list = query_grad.reshape(tile_rows, group_size * HEAD_DIM)
        key_parts.append(group_key)
        value_parts.append(group_value)
        query_grads.append(tile_list)
    query_grad_all = jnp.concatenate(query_grads, axis=1)
    partial_value = jnp.concatenate(key_parts + value_parts, axis=1)

    def shard_slot(offset):
        return partial_value[(REACH - offset) * shard_tokens : (REACH - offset + 1) * shard_tokens]

    summed = shard_slot(0)
    for offset in range(1, REACH + 1):
        summed = summed + shifted(shard_slot(offset).astype(jnp.bfloat16), "tm", -offset).astype(
            jnp.float32
        )
    keyval_grads = summed.astype(jnp.bfloat16)
    input_grad = contract_last(query_grad_all, query_full) + contract_last(
        keyval_grads, keyval_full
    )
    input_grad = input_grad.astype(jnp.bfloat16)
    weight_grad = grad_sum(contract_first(record_rows, keyval_grads))
    return (input_grad[None], weight_grad)


def solution(mesh):
    placed = (
        P("stream", "tm", None),
        P("stream", "tm", None),
        P("stream", None),
        P("stream", None),
        P("stream", None),
        P("stream"),
    )
    return jax.shard_map(
        per_device,
        mesh=mesh,
        in_specs=placed,
        out_specs=(P("stream", "tm", None), P("stream", None)),
        check_vma=False,
    )
```

```python
import jax
import jax.numpy as jnp
from jax import lax
from jax.sharding import PartitionSpec as P

HEADS = 16
KV_HEADS = 4
HEAD_DIM = 64
REACH = 4


def shifted(value, axis, steps):
    count = lax.axis_size(axis)
    leading, last = (max(0, -steps), min(count, count - steps))
    return lax.ppermute(value, axis, [(source, source + steps) for source in range(leading, last)])


def xor_swap(value, axis, bit):
    count = lax.axis_size(axis)
    return lax.ppermute(value, axis, [(source, source ^ (1 << bit)) for source in range(count)])


def tree_psum(value, axis):
    count = lax.axis_size(axis)
    bits = count.bit_length() - 1
    if count != 1 << bits or value.shape[0] % count:
        return lax.psum(value, axis)
    order = [b for b in (0, 2, 4, 1, 3, 5, 6) if b < bits] + list(range(7, bits))
    index = lax.axis_index(axis)
    current = value
    for bit in order:
        half = current.shape[0] // 2
        upper = ((index >> bit) & 1) == 1
        low, high = current[:half], current[half:]
        keep = jnp.where(upper, high, low)
        send = jnp.where(upper, low, high)
        current = keep + xor_swap(send, axis, bit)
    for bit in reversed(order):
        upper = ((index >> bit) & 1) == 1
        other = xor_swap(current, axis, bit)
        current = jnp.where(
            upper, jnp.concatenate([other, current]), jnp.concatenate([current, other])
        )
    return current


def halve_stage(value, axis, bit, wire):
    half = value.shape[0] // 2
    upper = ((lax.axis_index(axis) >> bit) & 1) == 1
    low, high = value[:half], value[half:]
    keep = jnp.where(upper, high, low).astype(jnp.float32)
    send = jnp.where(upper, low, high)
    return keep + xor_swap(send.astype(wire), axis, bit).astype(jnp.float32)


def double_stage(value, axis, bit):
    upper = ((lax.axis_index(axis) >> bit) & 1) == 1
    other = xor_swap(value, axis, bit)
    return jnp.where(upper, jnp.concatenate([other, value]), jnp.concatenate([value, other]))


def grad_sum(partial):
    stream_count = lax.axis_size("stream")
    tm_count = lax.axis_size("tm")
    stream_bits = stream_count.bit_length() - 1
    tm_bits = tm_count.bit_length() - 1
    if (
        stream_count != 1 << stream_bits
        or tm_count != 1 << tm_bits
        or partial.shape[0] % (2 * stream_count)
    ):
        shard = lax.psum_scatter(
            partial.astype(jnp.bfloat16), "stream", scatter_dimension=0, tiled=True
        ).astype(jnp.float32)
        return lax.psum(shard, "tm")
    stream_index = lax.axis_index("stream")
    current = partial.reshape((2,) * stream_bits + (-1,) + partial.shape[1:])
    for bit in range(stream_bits):
        axis_pos = stream_bits - 1 - bit
        upper = ((stream_index >> bit) & 1) == 1
        low = lax.index_in_dim(current, 0, axis_pos, keepdims=False)
        high = lax.index_in_dim(current, 1, axis_pos, keepdims=False)
        keep = jnp.where(upper, high, low).astype(jnp.float32)
        send = jnp.where(upper, low, high).astype(jnp.bfloat16)
        current = keep + xor_swap(send, "stream", bit).astype(jnp.float32)
    if tm_bits == 0:
        return current
    current = halve_stage(current, "tm", 0, jnp.float32)
    for bit in (2, 4, 1, 3, 5, 6) + tuple(range(7, tm_bits)):
        if bit < tm_bits:
            current = current + xor_swap(current, "tm", bit)
    return double_stage(current, "tm", 0)


def contract_last(left, right):
    return lax.dot_general(
        left, right, (((1,), (1,)), ((), ())), preferred_element_type=jnp.float32
    )


def contract_first(left, right):
    return lax.dot_general(
        left, right, (((0,), (0,)), ((), ())), preferred_element_type=jnp.float32
    )


def per_device(series, loss_grad, query_weight, keyval_weight, output_weight, lengths):
    record_rows = series[0]
    outer_grad = loss_grad[0]
    valid_count = lengths[0]
    shard_tokens = record_rows.shape[0]
    keyval_width = keyval_weight.shape[1]
    key_width = keyval_width // 2
    group_size = HEADS // KV_HEADS
    tile_rows = min(128, shard_tokens)
    key_span = REACH * shard_tokens + tile_rows
    score_scale = HEAD_DIM ** (-0.5)
    anchor = lax.axis_index("tm") * shard_tokens
    query_width = query_weight.shape[1]
    weights_local = jnp.concatenate([query_weight, keyval_weight, output_weight], axis=1)
    if lax.axis_size("tm") % 2 == 0 and weights_local.shape[1] % 256 == 0:
        half_width = weights_local.shape[1] // 2
        core = lax.axis_index("tm") % 2
        mine = lax.all_gather(
            lax.dynamic_slice_in_dim(weights_local, core * half_width, half_width, 1),
            "stream",
            axis=0,
            tiled=True,
        )
        other = xor_swap(mine, "tm", 0)
        weights_full = jnp.concatenate(
            [jnp.where(core == 0, mine, other), jnp.where(core == 0, other, mine)], axis=1
        )
    else:
        weights_full = lax.all_gather(weights_local, "stream", axis=0, tiled=True)
    query_full = weights_full[:, :query_width]
    keyval_full = weights_full[:, query_width : query_width + keyval_width]
    output_full = weights_full[:, query_width + keyval_width :]
    queries = jnp.dot(record_rows, query_full, preferred_element_type=jnp.float32).astype(
        jnp.bfloat16
    )
    keyvals = jnp.dot(record_rows, keyval_full, preferred_element_type=jnp.float32).astype(
        jnp.bfloat16
    )
    attn_grad = contract_last(outer_grad, output_full).astype(jnp.bfloat16)
    earlier = [shifted(keyvals, "tm", offset) for offset in range(REACH, 0, -1)]
    window_keyvals = jnp.concatenate(earlier + [keyvals], axis=0)
    key_parts = []
    value_parts = []
    query_grads = []
    for head_group in range(KV_HEADS):
        query_cols = slice(
            head_group * group_size * HEAD_DIM, (head_group + 1) * group_size * HEAD_DIM
        )
        key_cols = slice(head_group * HEAD_DIM, (head_group + 1) * HEAD_DIM)
        value_cols = slice(
            key_width + head_group * HEAD_DIM, key_width + (head_group + 1) * HEAD_DIM
        )
        group_key = None
        group_value = None
        query_tile = queries[0:tile_rows, query_cols].reshape(tile_rows, group_size, HEAD_DIM)
        key_tile = window_keyvals[0:key_span, key_cols]
        value_tile = window_keyvals[0:key_span, value_cols]
        query_pos = anchor + 0 + jnp.arange(tile_rows, dtype=jnp.int32)
        key_pos = anchor - REACH * shard_tokens + 0 + jnp.arange(key_span, dtype=jnp.int32)
        live_rows = query_pos < valid_count
        allowed = (key_pos[None, :] <= query_pos[:, None]) & (
            query_pos[:, None] - key_pos[None, :] < REACH * shard_tokens
        )
        allowed = (
            allowed
            & (key_pos[None, :] >= 0)
            & (key_pos[None, :] < valid_count)
            & live_rows[:, None]
        )
        scores = (
            jnp.einsum("qjd,kd->jqk", query_tile, key_tile, preferred_element_type=jnp.float32)
            * score_scale
        )
        masked = jnp.where(allowed, scores, -1e30)
        row_max = jnp.max(masked, axis=-1, keepdims=True)
        terms = jnp.where(allowed, jnp.exp(masked - row_max), 0.0)
        denom = jnp.sum(terms, axis=-1, keepdims=True)
        denom = jnp.where(live_rows[:, None], denom, 1.0)
        attn_probs = (terms / denom).astype(jnp.bfloat16)
        attn_tile = jnp.einsum(
            "jqk,kd->qjd", attn_probs, value_tile, preferred_element_type=jnp.float32
        ).astype(jnp.bfloat16)
        grad_tile = attn_grad[0:tile_rows, query_cols].reshape(tile_rows, group_size, HEAD_DIM)
        row_delta = jnp.sum(
            grad_tile.astype(jnp.float32) * attn_tile.astype(jnp.float32), axis=-1
        ).T[:, :, None]
        prob_grad = jnp.einsum(
            "qjd,kd->jqk", grad_tile, value_tile, preferred_element_type=jnp.float32
        )
        score_grad = (
            attn_probs.astype(jnp.float32) * (prob_grad - row_delta) * score_scale
        ).astype(jnp.bfloat16)
        query_grad = jnp.einsum(
            "jqk,kd->qjd", score_grad, key_tile, preferred_element_type=jnp.float32
        ).astype(jnp.bfloat16)
        key_grad = jnp.einsum(
            "jqk,qjd->kd", score_grad, query_tile, preferred_element_type=jnp.float32
        )
        value_grad = jnp.einsum(
            "jqk,qjd->kd", attn_probs, grad_tile, preferred_element_type=jnp.float32
        )
        group_key = key_grad
        group_value = value_grad
        tile_list = query_grad.reshape(tile_rows, group_size * HEAD_DIM)
        key_parts.append(group_key)
        value_parts.append(group_value)
        query_grads.append(tile_list)
    query_grad_all = jnp.concatenate(query_grads, axis=1)
    partial_value = jnp.concatenate(key_parts + value_parts, axis=1)

    def shard_slot(offset):
        return partial_value[(REACH - offset) * shard_tokens : (REACH - offset + 1) * shard_tokens]

    summed = shard_slot(0)
    for offset in range(1, REACH + 1):
        summed = summed + shifted(shard_slot(offset).astype(jnp.bfloat16), "tm", -offset).astype(
            jnp.float32
        )
    keyval_grads = summed.astype(jnp.bfloat16)
    input_grad = contract_last(query_grad_all, query_full) + contract_last(
        keyval_grads, keyval_full
    )
    input_grad = input_grad.astype(jnp.bfloat16)
    weight_grad = grad_sum(contract_first(record_rows, keyval_grads))
    return (input_grad[None], weight_grad)


def solution(mesh):
    placed = (
        P("stream", "tm", None),
        P("stream", "tm", None),
        P("stream", None),
        P("stream", None),
        P("stream", None),
        P("stream"),
    )
    return jax.shard_map(
        per_device,
        mesh=mesh,
        in_specs=placed,
        out_specs=(P("stream", "tm", None), P("stream", None)),
        check_vma=False,
    )
```

```python
import jax
import jax.numpy as jnp
from jax import lax
from jax.sharding import PartitionSpec as P

HEADS = 16
KV_HEADS = 4
HEAD_DIM = 64
REACH = 4


def shifted(value, axis, steps):
    count = lax.axis_size(axis)
    leading, last = (max(0, -steps), min(count, count - steps))
    return lax.ppermute(value, axis, [(source, source + steps) for source in range(leading, last)])


def xor_swap(value, axis, bit):
    count = lax.axis_size(axis)
    return lax.ppermute(value, axis, [(source, source ^ (1 << bit)) for source in range(count)])


def tree_psum(value, axis):
    count = lax.axis_size(axis)
    bits = count.bit_length() - 1
    if count != 1 << bits or value.shape[0] % count:
        return lax.psum(value, axis)
    order = [b for b in (0, 2, 4, 1, 3, 5, 6) if b < bits] + list(range(7, bits))
    index = lax.axis_index(axis)
    current = value
    for bit in order:
        half = current.shape[0] // 2
        upper = ((index >> bit) & 1) == 1
        low, high = current[:half], current[half:]
        keep = jnp.where(upper, high, low)
        send = jnp.where(upper, low, high)
        current = keep + xor_swap(send, axis, bit)
    for bit in reversed(order):
        upper = ((index >> bit) & 1) == 1
        other = xor_swap(current, axis, bit)
        current = jnp.where(
            upper, jnp.concatenate([other, current]), jnp.concatenate([current, other])
        )
    return current


def halve_stage(value, axis, bit, wire):
    half = value.shape[0] // 2
    upper = ((lax.axis_index(axis) >> bit) & 1) == 1
    low, high = value[:half], value[half:]
    keep = jnp.where(upper, high, low).astype(jnp.float32)
    send = jnp.where(upper, low, high)
    return keep + xor_swap(send.astype(wire), axis, bit).astype(jnp.float32)


def double_stage(value, axis, bit):
    upper = ((lax.axis_index(axis) >> bit) & 1) == 1
    other = xor_swap(value, axis, bit)
    return jnp.where(upper, jnp.concatenate([other, value]), jnp.concatenate([value, other]))


def grad_sum(partial):
    stream_count = lax.axis_size("stream")
    tm_count = lax.axis_size("tm")
    stream_bits = stream_count.bit_length() - 1
    tm_bits = tm_count.bit_length() - 1
    if (
        stream_count != 1 << stream_bits
        or tm_count != 1 << tm_bits
        or partial[0].shape[1] % (2 * stream_count)
    ):
        shard = lax.psum_scatter(
            contract_first(*partial).astype(jnp.bfloat16), "stream", scatter_dimension=0, tiled=True
        ).astype(jnp.float32)
        return lax.psum(shard, "tm")
    stream_index = lax.axis_index("stream")
    rows, grads = partial
    tokens, features = rows.shape
    if stream_bits == 0:
        current = contract_first(rows, grads)
    else:
        paired = rows.reshape(tokens, stream_count // 2, 2, features // stream_count)
        even = paired[:, :, 0].reshape(tokens, features // 2)
        odd = paired[:, :, 1].reshape(tokens, features // 2)
        upper = (stream_index & 1) == 1
        keep = contract_first(jnp.where(upper, odd, even), grads)
        send = contract_first(jnp.where(upper, even, odd), grads).astype(jnp.bfloat16)
        current = keep + xor_swap(send, "stream", 0).astype(jnp.float32)
    for bit in reversed(range(1, stream_bits)):
        current = halve_stage(current, "stream", bit, jnp.bfloat16)
    if tm_bits == 0:
        return current
    current = halve_stage(current, "tm", 0, jnp.float32)
    for bit in (2, 4, 1, 3, 5, 6) + tuple(range(7, tm_bits)):
        if bit < tm_bits:
            current = current + xor_swap(current, "tm", bit)
    return double_stage(current, "tm", 0)


def contract_last(left, right):
    return lax.dot_general(
        left, right, (((1,), (1,)), ((), ())), preferred_element_type=jnp.float32
    )


def contract_first(left, right):
    return lax.dot_general(
        left, right, (((0,), (0,)), ((), ())), preferred_element_type=jnp.float32
    )


def per_device(series, loss_grad, query_weight, keyval_weight, output_weight, lengths):
    record_rows = series[0]
    outer_grad = loss_grad[0]
    valid_count = lengths[0]
    shard_tokens = record_rows.shape[0]
    keyval_width = keyval_weight.shape[1]
    key_width = keyval_width // 2
    group_size = HEADS // KV_HEADS
    tile_rows = min(128, shard_tokens)
    key_span = REACH * shard_tokens + tile_rows
    score_scale = HEAD_DIM ** (-0.5)
    anchor = lax.axis_index("tm") * shard_tokens
    query_width = query_weight.shape[1]
    weights_local = jnp.concatenate([query_weight, keyval_weight, output_weight], axis=1)
    if lax.axis_size("tm") % 2 == 0 and weights_local.shape[1] % 256 == 0:
        half_width = weights_local.shape[1] // 2
        core = lax.axis_index("tm") % 2
        mine = lax.all_gather(
            lax.dynamic_slice_in_dim(weights_local, core * half_width, half_width, 1),
            "stream",
            axis=0,
            tiled=True,
        )
        other = xor_swap(mine, "tm", 0)
        weights_full = jnp.concatenate(
            [jnp.where(core == 0, mine, other), jnp.where(core == 0, other, mine)], axis=1
        )
    else:
        weights_full = lax.all_gather(weights_local, "stream", axis=0, tiled=True)
    query_full = weights_full[:, :query_width]
    keyval_full = weights_full[:, query_width : query_width + keyval_width]
    output_full = weights_full[:, query_width + keyval_width :]
    queries = jnp.dot(record_rows, query_full, preferred_element_type=jnp.float32).astype(
        jnp.bfloat16
    )
    keyvals = jnp.dot(record_rows, keyval_full, preferred_element_type=jnp.float32).astype(
        jnp.bfloat16
    )
    attn_grad = contract_last(outer_grad, output_full).astype(jnp.bfloat16)
    earlier = [shifted(keyvals, "tm", offset) for offset in range(REACH, 0, -1)]
    window_keyvals = jnp.concatenate(earlier + [keyvals], axis=0)
    key_parts = []
    value_parts = []
    query_grads = []
    for head_group in range(KV_HEADS):
        query_cols = slice(
            head_group * group_size * HEAD_DIM, (head_group + 1) * group_size * HEAD_DIM
        )
        key_cols = slice(head_group * HEAD_DIM, (head_group + 1) * HEAD_DIM)
        value_cols = slice(
            key_width + head_group * HEAD_DIM, key_width + (head_group + 1) * HEAD_DIM
        )
        group_key = None
        group_value = None
        query_tile = queries[0:tile_rows, query_cols].reshape(tile_rows, group_size, HEAD_DIM)
        key_tile = window_keyvals[0:key_span, key_cols]
        value_tile = window_keyvals[0:key_span, value_cols]
        query_pos = anchor + 0 + jnp.arange(tile_rows, dtype=jnp.int32)
        key_pos = anchor - REACH * shard_tokens + 0 + jnp.arange(key_span, dtype=jnp.int32)
        live_rows = query_pos < valid_count
        allowed = (key_pos[None, :] <= query_pos[:, None]) & (
            query_pos[:, None] - key_pos[None, :] < REACH * shard_tokens
        )
        allowed = (
            allowed
            & (key_pos[None, :] >= 0)
            & (key_pos[None, :] < valid_count)
            & live_rows[:, None]
        )
        scores = (
            jnp.einsum("qjd,kd->jqk", query_tile, key_tile, preferred_element_type=jnp.float32)
            * score_scale
        )
        masked = jnp.where(allowed, scores, -1e30)
        row_max = jnp.max(masked, axis=-1, keepdims=True)
        terms = jnp.where(allowed, jnp.exp(masked - row_max), 0.0)
        denom = jnp.sum(terms, axis=-1, keepdims=True)
        denom = jnp.where(live_rows[:, None], denom, 1.0)
        attn_probs = (terms / denom).astype(jnp.bfloat16)
        attn_tile = jnp.einsum(
            "jqk,kd->qjd", attn_probs, value_tile, preferred_element_type=jnp.float32
        ).astype(jnp.bfloat16)
        grad_tile = attn_grad[0:tile_rows, query_cols].reshape(tile_rows, group_size, HEAD_DIM)
        row_delta = jnp.sum(
            grad_tile.astype(jnp.float32) * attn_tile.astype(jnp.float32), axis=-1
        ).T[:, :, None]
        prob_grad = jnp.einsum(
            "qjd,kd->jqk", grad_tile, value_tile, preferred_element_type=jnp.float32
        )
        score_grad = (
            attn_probs.astype(jnp.float32) * (prob_grad - row_delta) * score_scale
        ).astype(jnp.bfloat16)
        query_grad = jnp.einsum(
            "jqk,kd->qjd", score_grad, key_tile, preferred_element_type=jnp.float32
        ).astype(jnp.bfloat16)
        key_grad = jnp.einsum(
            "jqk,qjd->kd", score_grad, query_tile, preferred_element_type=jnp.float32
        )
        value_grad = jnp.einsum(
            "jqk,qjd->kd", attn_probs, grad_tile, preferred_element_type=jnp.float32
        )
        group_key = key_grad
        group_value = value_grad
        tile_list = query_grad.reshape(tile_rows, group_size * HEAD_DIM)
        key_parts.append(group_key)
        value_parts.append(group_value)
        query_grads.append(tile_list)
    query_grad_all = jnp.concatenate(query_grads, axis=1)
    partial_value = jnp.concatenate(key_parts + value_parts, axis=1)

    def shard_slot(offset):
        return partial_value[(REACH - offset) * shard_tokens : (REACH - offset + 1) * shard_tokens]

    summed = shard_slot(0)
    for offset in range(1, REACH + 1):
        summed = summed + shifted(shard_slot(offset).astype(jnp.bfloat16), "tm", -offset).astype(
            jnp.float32
        )
    keyval_grads = summed.astype(jnp.bfloat16)
    input_grad = contract_last(query_grad_all, query_full) + contract_last(
        keyval_grads, keyval_full
    )
    input_grad = input_grad.astype(jnp.bfloat16)
    weight_grad = grad_sum((record_rows, keyval_grads))
    return (input_grad[None], weight_grad)


def solution(mesh):
    placed = (
        P("stream", "tm", None),
        P("stream", "tm", None),
        P("stream", None),
        P("stream", None),
        P("stream", None),
        P("stream"),
    )
    return jax.shard_map(
        per_device,
        mesh=mesh,
        in_specs=placed,
        out_specs=(P("stream", "tm", None), P("stream", None)),
        check_vma=False,
    )
```

```python
import jax
import jax.numpy as jnp
from jax import lax
from jax.sharding import PartitionSpec as P

HEADS = 16
KV_HEADS = 4
HEAD_DIM = 64
REACH = 4


def shifted(value, axis, steps):
    count = lax.axis_size(axis)
    leading, last = (max(0, -steps), min(count, count - steps))
    return lax.ppermute(value, axis, [(source, source + steps) for source in range(leading, last)])


def xor_swap(value, axis, bit):
    count = lax.axis_size(axis)
    return lax.ppermute(value, axis, [(source, source ^ (1 << bit)) for source in range(count)])


def tree_psum(value, axis):
    count = lax.axis_size(axis)
    bits = count.bit_length() - 1
    if count != 1 << bits or value.shape[0] % count:
        return lax.psum(value, axis)
    order = [b for b in (0, 2, 4, 1, 3, 5, 6) if b < bits] + list(range(7, bits))
    index = lax.axis_index(axis)
    current = value
    for bit in order:
        half = current.shape[0] // 2
        upper = ((index >> bit) & 1) == 1
        low, high = current[:half], current[half:]
        keep = jnp.where(upper, high, low)
        send = jnp.where(upper, low, high)
        current = keep + xor_swap(send, axis, bit)
    for bit in reversed(order):
        upper = ((index >> bit) & 1) == 1
        other = xor_swap(current, axis, bit)
        current = jnp.where(
            upper, jnp.concatenate([other, current]), jnp.concatenate([current, other])
        )
    return current


def halve_stage(value, axis, bit, wire):
    half = value.shape[0] // 2
    upper = ((lax.axis_index(axis) >> bit) & 1) == 1
    low, high = value[:half], value[half:]
    keep = jnp.where(upper, high, low).astype(jnp.float32)
    send = jnp.where(upper, low, high)
    return keep + xor_swap(send.astype(wire), axis, bit).astype(jnp.float32)


def double_stage(value, axis, bit):
    upper = ((lax.axis_index(axis) >> bit) & 1) == 1
    other = xor_swap(value, axis, bit)
    return jnp.where(upper, jnp.concatenate([other, value]), jnp.concatenate([value, other]))


NEAR_BITS = (0, 2, 4)


def grad_sum(partial):
    stream_count = lax.axis_size("stream")
    tm_count = lax.axis_size("tm")
    stream_bits = stream_count.bit_length() - 1
    tm_bits = tm_count.bit_length() - 1
    if (
        stream_count != 1 << stream_bits
        or tm_count != 1 << tm_bits
        or partial[0].shape[1] % (2 * stream_count)
    ):
        shard = lax.psum_scatter(
            contract_first(*partial).astype(jnp.bfloat16), "stream", scatter_dimension=0, tiled=True
        ).astype(jnp.float32)
        return lax.psum(shard, "tm")
    stream_index = lax.axis_index("stream")
    rows, grads = partial
    tokens, features = rows.shape
    if stream_bits == 0:
        current = contract_first(rows, grads)
    else:
        paired = rows.reshape(tokens, stream_count // 2, 2, features // stream_count)
        even = paired[:, :, 0].reshape(tokens, features // 2)
        odd = paired[:, :, 1].reshape(tokens, features // 2)
        upper = (stream_index & 1) == 1
        keep = contract_first(jnp.where(upper, odd, even), grads)
        send = contract_first(jnp.where(upper, even, odd), grads).astype(jnp.bfloat16)
        current = keep + xor_swap(send, "stream", 0).astype(jnp.float32)
    for bit in reversed(range(1, stream_bits)):
        current = halve_stage(current, "stream", bit, jnp.bfloat16)
    if tm_bits == 0:
        return current
    near = [bit for bit in NEAR_BITS if bit < tm_bits and current.shape[0] % 2 == 0]
    near = near[: max(0, (current.shape[0]).bit_length() - 1)]
    for bit in near:
        current = halve_stage(current, "tm", bit, jnp.float32)
    for bit in range(tm_bits):
        if bit not in near:
            current = current + xor_swap(current, "tm", bit)
    for bit in reversed(near):
        current = double_stage(current, "tm", bit)
    return current


def contract_last(left, right):
    return lax.dot_general(
        left, right, (((1,), (1,)), ((), ())), preferred_element_type=jnp.float32
    )


def contract_first(left, right):
    return lax.dot_general(
        left, right, (((0,), (0,)), ((), ())), preferred_element_type=jnp.float32
    )


def per_device(series, loss_grad, query_weight, keyval_weight, output_weight, lengths):
    record_rows = series[0]
    outer_grad = loss_grad[0]
    valid_count = lengths[0]
    shard_tokens = record_rows.shape[0]
    keyval_width = keyval_weight.shape[1]
    key_width = keyval_width // 2
    group_size = HEADS // KV_HEADS
    tile_rows = min(128, shard_tokens)
    key_span = REACH * shard_tokens + tile_rows
    score_scale = HEAD_DIM ** (-0.5)
    anchor = lax.axis_index("tm") * shard_tokens
    query_width = query_weight.shape[1]
    weights_local = jnp.concatenate([query_weight, keyval_weight, output_weight], axis=1)
    if lax.axis_size("tm") % 2 == 0 and weights_local.shape[1] % 256 == 0:
        half_width = weights_local.shape[1] // 2
        core = lax.axis_index("tm") % 2
        mine = lax.all_gather(
            lax.dynamic_slice_in_dim(weights_local, core * half_width, half_width, 1),
            "stream",
            axis=0,
            tiled=True,
        )
        other = xor_swap(mine, "tm", 0)
        weights_full = jnp.concatenate(
            [jnp.where(core == 0, mine, other), jnp.where(core == 0, other, mine)], axis=1
        )
    else:
        weights_full = lax.all_gather(weights_local, "stream", axis=0, tiled=True)
    query_full = weights_full[:, :query_width]
    keyval_full = weights_full[:, query_width : query_width + keyval_width]
    output_full = weights_full[:, query_width + keyval_width :]
    queries = jnp.dot(record_rows, query_full, preferred_element_type=jnp.float32).astype(
        jnp.bfloat16
    )
    keyvals = jnp.dot(record_rows, keyval_full, preferred_element_type=jnp.float32).astype(
        jnp.bfloat16
    )
    attn_grad = contract_last(outer_grad, output_full).astype(jnp.bfloat16)
    earlier = [shifted(keyvals, "tm", offset) for offset in range(REACH, 0, -1)]
    window_keyvals = jnp.concatenate(earlier + [keyvals], axis=0)
    key_parts = []
    value_parts = []
    query_grads = []
    for head_group in range(KV_HEADS):
        query_cols = slice(
            head_group * group_size * HEAD_DIM, (head_group + 1) * group_size * HEAD_DIM
        )
        key_cols = slice(head_group * HEAD_DIM, (head_group + 1) * HEAD_DIM)
        value_cols = slice(
            key_width + head_group * HEAD_DIM, key_width + (head_group + 1) * HEAD_DIM
        )
        group_key = None
        group_value = None
        query_tile = queries[0:tile_rows, query_cols].reshape(tile_rows, group_size, HEAD_DIM)
        key_tile = window_keyvals[0:key_span, key_cols]
        value_tile = window_keyvals[0:key_span, value_cols]
        query_pos = anchor + 0 + jnp.arange(tile_rows, dtype=jnp.int32)
        key_pos = anchor - REACH * shard_tokens + 0 + jnp.arange(key_span, dtype=jnp.int32)
        live_rows = query_pos < valid_count
        allowed = (key_pos[None, :] <= query_pos[:, None]) & (
            query_pos[:, None] - key_pos[None, :] < REACH * shard_tokens
        )
        allowed = (
            allowed
            & (key_pos[None, :] >= 0)
            & (key_pos[None, :] < valid_count)
            & live_rows[:, None]
        )
        scores = (
            jnp.einsum("qjd,kd->jqk", query_tile, key_tile, preferred_element_type=jnp.float32)
            * score_scale
        )
        masked = jnp.where(allowed, scores, -1e30)
        row_max = jnp.max(masked, axis=-1, keepdims=True)
        terms = jnp.where(allowed, jnp.exp(masked - row_max), 0.0)
        denom = jnp.sum(terms, axis=-1, keepdims=True)
        denom = jnp.where(live_rows[:, None], denom, 1.0)
        attn_probs = (terms / denom).astype(jnp.bfloat16)
        attn_tile = jnp.einsum(
            "jqk,kd->qjd", attn_probs, value_tile, preferred_element_type=jnp.float32
        ).astype(jnp.bfloat16)
        grad_tile = attn_grad[0:tile_rows, query_cols].reshape(tile_rows, group_size, HEAD_DIM)
        row_delta = jnp.sum(
            grad_tile.astype(jnp.float32) * attn_tile.astype(jnp.float32), axis=-1
        ).T[:, :, None]
        prob_grad = jnp.einsum(
            "qjd,kd->jqk", grad_tile, value_tile, preferred_element_type=jnp.float32
        )
        score_grad = (
            attn_probs.astype(jnp.float32) * (prob_grad - row_delta) * score_scale
        ).astype(jnp.bfloat16)
        query_grad = jnp.einsum(
            "jqk,kd->qjd", score_grad, key_tile, preferred_element_type=jnp.float32
        ).astype(jnp.bfloat16)
        key_grad = jnp.einsum(
            "jqk,qjd->kd", score_grad, query_tile, preferred_element_type=jnp.float32
        )
        value_grad = jnp.einsum(
            "jqk,qjd->kd", attn_probs, grad_tile, preferred_element_type=jnp.float32
        )
        group_key = key_grad
        group_value = value_grad
        tile_list = query_grad.reshape(tile_rows, group_size * HEAD_DIM)
        key_parts.append(group_key)
        value_parts.append(group_value)
        query_grads.append(tile_list)
    query_grad_all = jnp.concatenate(query_grads, axis=1)
    partial_value = jnp.concatenate(key_parts + value_parts, axis=1)

    def shard_slot(offset):
        return partial_value[(REACH - offset) * shard_tokens : (REACH - offset + 1) * shard_tokens]

    summed = shard_slot(0)
    for offset in range(1, REACH + 1):
        summed = summed + shifted(shard_slot(offset).astype(jnp.bfloat16), "tm", -offset).astype(
            jnp.float32
        )
    keyval_grads = summed.astype(jnp.bfloat16)
    input_grad = contract_last(query_grad_all, query_full) + contract_last(
        keyval_grads, keyval_full
    )
    input_grad = input_grad.astype(jnp.bfloat16)
    weight_grad = grad_sum((record_rows, keyval_grads))
    return (input_grad[None], weight_grad)


def solution(mesh):
    placed = (
        P("stream", "tm", None),
        P("stream", "tm", None),
        P("stream", None),
        P("stream", None),
        P("stream", None),
        P("stream"),
    )
    return jax.shard_map(
        per_device,
        mesh=mesh,
        in_specs=placed,
        out_specs=(P("stream", "tm", None), P("stream", None)),
        check_vma=False,
    )
```

```python
import jax
import jax.numpy as jnp
from jax import lax
from jax.sharding import PartitionSpec as P

HEADS = 16
KV_HEADS = 4
HEAD_DIM = 64
REACH = 4


def shifted(value, axis, steps):
    count = lax.axis_size(axis)
    leading, last = (max(0, -steps), min(count, count - steps))
    return lax.ppermute(value, axis, [(source, source + steps) for source in range(leading, last)])


def xor_swap(value, axis, bit):
    count = lax.axis_size(axis)
    return lax.ppermute(value, axis, [(source, source ^ (1 << bit)) for source in range(count)])


def tree_psum(value, axis):
    count = lax.axis_size(axis)
    bits = count.bit_length() - 1
    if count != 1 << bits or value.shape[0] % count:
        return lax.psum(value, axis)
    order = [b for b in (0, 2, 4, 1, 3, 5, 6) if b < bits] + list(range(7, bits))
    index = lax.axis_index(axis)
    current = value
    for bit in order:
        half = current.shape[0] // 2
        upper = ((index >> bit) & 1) == 1
        low, high = current[:half], current[half:]
        keep = jnp.where(upper, high, low)
        send = jnp.where(upper, low, high)
        current = keep + xor_swap(send, axis, bit)
    for bit in reversed(order):
        upper = ((index >> bit) & 1) == 1
        other = xor_swap(current, axis, bit)
        current = jnp.where(
            upper, jnp.concatenate([other, current]), jnp.concatenate([current, other])
        )
    return current


def halve_stage(value, axis, bit, wire):
    half = value.shape[0] // 2
    upper = ((lax.axis_index(axis) >> bit) & 1) == 1
    low, high = value[:half], value[half:]
    keep = jnp.where(upper, high, low).astype(jnp.float32)
    send = jnp.where(upper, low, high)
    return keep + xor_swap(send.astype(wire), axis, bit).astype(jnp.float32)


def double_stage(value, axis, bit):
    upper = ((lax.axis_index(axis) >> bit) & 1) == 1
    other = xor_swap(value, axis, bit)
    return jnp.where(upper, jnp.concatenate([other, value]), jnp.concatenate([value, other]))


NEAR_BITS = (2, 4)


def grad_sum(partial):
    stream_count = lax.axis_size("stream")
    tm_count = lax.axis_size("tm")
    stream_bits = stream_count.bit_length() - 1
    tm_bits = tm_count.bit_length() - 1
    rows, grads = partial
    tokens, features = rows.shape
    if (
        stream_count != 1 << stream_bits
        or tm_count != 1 << tm_bits
        or stream_bits == 0
        or tm_bits == 0
        or features % (2 * stream_count)
        or grads.shape[1] % 256
    ):
        shard = lax.psum_scatter(
            contract_first(rows, grads).astype(jnp.bfloat16), "stream", scatter_dimension=0, tiled=True
        ).astype(jnp.float32)
        return lax.psum(shard, "tm")
    stream_index = lax.axis_index("stream")
    core = lax.axis_index("tm") % 2
    half_cols = grads.shape[1] // 2
    paired = rows.reshape(tokens, stream_count // 2, 2, features // stream_count)
    even = paired[:, :, 0].reshape(tokens, features // 2)
    odd = paired[:, :, 1].reshape(tokens, features // 2)
    upper = (stream_index & 1) == 1
    ordered = jnp.concatenate([jnp.where(upper, odd, even), jnp.where(upper, even, odd)], axis=1)
    mine_cols = lax.dynamic_slice_in_dim(grads, core * half_cols, half_cols, 1)
    other_cols = lax.dynamic_slice_in_dim(grads, (1 - core) * half_cols, half_cols, 1)
    current = contract_first(ordered, mine_cols) + xor_swap(
        contract_first(ordered, other_cols), "tm", 0
    )
    half_rows = features // 2
    current = current[:half_rows] + xor_swap(
        current[half_rows:].astype(jnp.bfloat16), "stream", 0
    ).astype(jnp.float32)
    for bit in reversed(range(1, stream_bits)):
        current = halve_stage(current, "stream", bit, jnp.bfloat16)
    near = [bit for bit in NEAR_BITS if bit < tm_bits]
    near = near[: max(0, current.shape[0].bit_length() - 1)]
    for bit in near:
        current = halve_stage(current, "tm", bit, jnp.float32)
    for bit in range(1, tm_bits):
        if bit not in near:
            current = current + xor_swap(current, "tm", bit)
    for bit in reversed(near):
        current = double_stage(current, "tm", bit)
    other = xor_swap(current, "tm", 0)
    return jnp.where(
        core == 1,
        jnp.concatenate([other, current], axis=1),
        jnp.concatenate([current, other], axis=1),
    )


def contract_last(left, right):
    return lax.dot_general(
        left, right, (((1,), (1,)), ((), ())), preferred_element_type=jnp.float32
    )


def contract_first(left, right):
    return lax.dot_general(
        left, right, (((0,), (0,)), ((), ())), preferred_element_type=jnp.float32
    )


def per_device(series, loss_grad, query_weight, keyval_weight, output_weight, lengths):
    record_rows = series[0]
    outer_grad = loss_grad[0]
    valid_count = lengths[0]
    shard_tokens = record_rows.shape[0]
    keyval_width = keyval_weight.shape[1]
    key_width = keyval_width // 2
    group_size = HEADS // KV_HEADS
    tile_rows = min(128, shard_tokens)
    key_span = REACH * shard_tokens + tile_rows
    score_scale = HEAD_DIM ** (-0.5)
    anchor = lax.axis_index("tm") * shard_tokens
    query_width = query_weight.shape[1]
    weights_local = jnp.concatenate([query_weight, keyval_weight, output_weight], axis=1)
    if lax.axis_size("tm") % 2 == 0 and weights_local.shape[1] % 256 == 0:
        half_width = weights_local.shape[1] // 2
        core = lax.axis_index("tm") % 2
        mine = lax.all_gather(
            lax.dynamic_slice_in_dim(weights_local, core * half_width, half_width, 1),
            "stream",
            axis=0,
            tiled=True,
        )
        other = xor_swap(mine, "tm", 0)
        weights_full = jnp.concatenate(
            [jnp.where(core == 0, mine, other), jnp.where(core == 0, other, mine)], axis=1
        )
    else:
        weights_full = lax.all_gather(weights_local, "stream", axis=0, tiled=True)
    query_full = weights_full[:, :query_width]
    keyval_full = weights_full[:, query_width : query_width + keyval_width]
    output_full = weights_full[:, query_width + keyval_width :]
    queries = jnp.dot(record_rows, query_full, preferred_element_type=jnp.float32).astype(
        jnp.bfloat16
    )
    keyvals = jnp.dot(record_rows, keyval_full, preferred_element_type=jnp.float32).astype(
        jnp.bfloat16
    )
    attn_grad = contract_last(outer_grad, output_full).astype(jnp.bfloat16)
    earlier = [shifted(keyvals, "tm", offset) for offset in range(REACH, 0, -1)]
    window_keyvals = jnp.concatenate(earlier + [keyvals], axis=0)
    key_parts = []
    value_parts = []
    query_grads = []
    for head_group in range(KV_HEADS):
        query_cols = slice(
            head_group * group_size * HEAD_DIM, (head_group + 1) * group_size * HEAD_DIM
        )
        key_cols = slice(head_group * HEAD_DIM, (head_group + 1) * HEAD_DIM)
        value_cols = slice(
            key_width + head_group * HEAD_DIM, key_width + (head_group + 1) * HEAD_DIM
        )
        group_key = None
        group_value = None
        query_tile = queries[0:tile_rows, query_cols].reshape(tile_rows, group_size, HEAD_DIM)
        key_tile = window_keyvals[0:key_span, key_cols]
        value_tile = window_keyvals[0:key_span, value_cols]
        query_pos = anchor + 0 + jnp.arange(tile_rows, dtype=jnp.int32)
        key_pos = anchor - REACH * shard_tokens + 0 + jnp.arange(key_span, dtype=jnp.int32)
        live_rows = query_pos < valid_count
        allowed = (key_pos[None, :] <= query_pos[:, None]) & (
            query_pos[:, None] - key_pos[None, :] < REACH * shard_tokens
        )
        allowed = (
            allowed
            & (key_pos[None, :] >= 0)
            & (key_pos[None, :] < valid_count)
            & live_rows[:, None]
        )
        scores = (
            jnp.einsum("qjd,kd->jqk", query_tile, key_tile, preferred_element_type=jnp.float32)
            * score_scale
        )
        masked = jnp.where(allowed, scores, -1e30)
        row_max = jnp.max(masked, axis=-1, keepdims=True)
        terms = jnp.where(allowed, jnp.exp(masked - row_max), 0.0)
        denom = jnp.sum(terms, axis=-1, keepdims=True)
        denom = jnp.where(live_rows[:, None], denom, 1.0)
        attn_probs = (terms / denom).astype(jnp.bfloat16)
        attn_tile = jnp.einsum(
            "jqk,kd->qjd", attn_probs, value_tile, preferred_element_type=jnp.float32
        ).astype(jnp.bfloat16)
        grad_tile = attn_grad[0:tile_rows, query_cols].reshape(tile_rows, group_size, HEAD_DIM)
        row_delta = jnp.sum(
            grad_tile.astype(jnp.float32) * attn_tile.astype(jnp.float32), axis=-1
        ).T[:, :, None]
        prob_grad = jnp.einsum(
            "qjd,kd->jqk", grad_tile, value_tile, preferred_element_type=jnp.float32
        )
        score_grad = (
            attn_probs.astype(jnp.float32) * (prob_grad - row_delta) * score_scale
        ).astype(jnp.bfloat16)
        query_grad = jnp.einsum(
            "jqk,kd->qjd", score_grad, key_tile, preferred_element_type=jnp.float32
        ).astype(jnp.bfloat16)
        key_grad = jnp.einsum(
            "jqk,qjd->kd", score_grad, query_tile, preferred_element_type=jnp.float32
        )
        value_grad = jnp.einsum(
            "jqk,qjd->kd", attn_probs, grad_tile, preferred_element_type=jnp.float32
        )
        group_key = key_grad
        group_value = value_grad
        tile_list = query_grad.reshape(tile_rows, group_size * HEAD_DIM)
        key_parts.append(group_key)
        value_parts.append(group_value)
        query_grads.append(tile_list)
    query_grad_all = jnp.concatenate(query_grads, axis=1)
    partial_value = jnp.concatenate(key_parts + value_parts, axis=1)

    def shard_slot(offset):
        return partial_value[(REACH - offset) * shard_tokens : (REACH - offset + 1) * shard_tokens]

    summed = shard_slot(0)
    for offset in range(1, REACH + 1):
        summed = summed + shifted(shard_slot(offset).astype(jnp.bfloat16), "tm", -offset).astype(
            jnp.float32
        )
    keyval_grads = summed.astype(jnp.bfloat16)
    input_grad = contract_last(query_grad_all, query_full) + contract_last(
        keyval_grads, keyval_full
    )
    input_grad = input_grad.astype(jnp.bfloat16)
    weight_grad = grad_sum((record_rows, keyval_grads))
    return (input_grad[None], weight_grad)


def solution(mesh):
    placed = (
        P("stream", "tm", None),
        P("stream", "tm", None),
        P("stream", None),
        P("stream", None),
        P("stream", None),
        P("stream"),
    )
    return jax.shard_map(
        per_device,
        mesh=mesh,
        in_specs=placed,
        out_specs=(P("stream", "tm", None), P("stream", None)),
        check_vma=False,
    )
```

```python
import jax
import jax.numpy as jnp
from jax import lax
from jax.sharding import PartitionSpec as P

HEADS = 16
KV_HEADS = 4
HEAD_DIM = 64
REACH = 4


def shifted(value, axis, steps):
    count = lax.axis_size(axis)
    leading, last = (max(0, -steps), min(count, count - steps))
    return lax.ppermute(value, axis, [(source, source + steps) for source in range(leading, last)])


def xor_swap(value, axis, bit):
    count = lax.axis_size(axis)
    return lax.ppermute(value, axis, [(source, source ^ (1 << bit)) for source in range(count)])


def tree_psum(value, axis):
    count = lax.axis_size(axis)
    bits = count.bit_length() - 1
    if count != 1 << bits or value.shape[0] % count:
        return lax.psum(value, axis)
    order = [b for b in (0, 2, 4, 1, 3, 5, 6) if b < bits] + list(range(7, bits))
    index = lax.axis_index(axis)
    current = value
    for bit in order:
        half = current.shape[0] // 2
        upper = ((index >> bit) & 1) == 1
        low, high = current[:half], current[half:]
        keep = jnp.where(upper, high, low)
        send = jnp.where(upper, low, high)
        current = keep + xor_swap(send, axis, bit)
    for bit in reversed(order):
        upper = ((index >> bit) & 1) == 1
        other = xor_swap(current, axis, bit)
        current = jnp.where(
            upper, jnp.concatenate([other, current]), jnp.concatenate([current, other])
        )
    return current


def halve_stage(value, axis, bit, wire):
    half = value.shape[0] // 2
    upper = ((lax.axis_index(axis) >> bit) & 1) == 1
    low, high = value[:half], value[half:]
    keep = jnp.where(upper, high, low).astype(jnp.float32)
    send = jnp.where(upper, low, high)
    return keep + xor_swap(send.astype(wire), axis, bit).astype(jnp.float32)


def double_stage(value, axis, bit):
    upper = ((lax.axis_index(axis) >> bit) & 1) == 1
    other = xor_swap(value, axis, bit)
    return jnp.where(upper, jnp.concatenate([other, value]), jnp.concatenate([value, other]))


NEAR_BITS = (2, 4)


def grad_sum(partial):
    stream_count = lax.axis_size("stream")
    tm_count = lax.axis_size("tm")
    stream_bits = stream_count.bit_length() - 1
    tm_bits = tm_count.bit_length() - 1
    rows, grads = partial
    tokens, features = rows.shape
    if (
        stream_count != 1 << stream_bits
        or tm_count != 1 << tm_bits
        or stream_bits == 0
        or tm_bits == 0
        or features % (2 * stream_count)
        or grads.shape[1] % 256
    ):
        shard = lax.psum_scatter(
            contract_first(rows, grads).astype(jnp.bfloat16), "stream", scatter_dimension=0, tiled=True
        ).astype(jnp.float32)
        return lax.psum(shard, "tm")
    stream_index = lax.axis_index("stream")
    core = lax.axis_index("tm") % 2
    half_cols = grads.shape[1] // 2
    paired = rows.reshape(tokens, stream_count // 2, 2, features // stream_count)
    even = paired[:, :, 0].reshape(tokens, features // 2)
    odd = paired[:, :, 1].reshape(tokens, features // 2)
    upper = (stream_index & 1) == 1
    ordered = jnp.concatenate([jnp.where(upper, odd, even), jnp.where(upper, even, odd)], axis=1)
    mine_cols = lax.dynamic_slice_in_dim(grads, core * half_cols, half_cols, 1)
    other_cols = lax.dynamic_slice_in_dim(grads, (1 - core) * half_cols, half_cols, 1)
    current = contract_first(ordered, mine_cols) + xor_swap(
        contract_first(ordered, other_cols), "tm", 0
    )
    half_rows = features // 2
    current = current[:half_rows] + xor_swap(
        current[half_rows:].astype(jnp.bfloat16), "stream", 0
    ).astype(jnp.float32)
    for bit in reversed(range(1, stream_bits)):
        current = halve_stage(current, "stream", bit, jnp.bfloat16)
    near = [bit for bit in NEAR_BITS if bit < tm_bits]
    near = near[: max(0, current.shape[0].bit_length() - 1)]
    for bit in near:
        current = halve_stage(current, "tm", bit, jnp.float32)
    for bit in range(1, tm_bits):
        if bit not in near:
            current = current + xor_swap(current, "tm", bit)
    for bit in reversed(near):
        current = double_stage(current, "tm", bit)
    other = xor_swap(current, "tm", 0)
    return jnp.where(
        core == 1,
        jnp.concatenate([other, current], axis=1),
        jnp.concatenate([current, other], axis=1),
    )


def ring_source(linear, shift, stream_count):
    tm_index, stream_index = divmod(linear, stream_count)
    ring = 2 * stream_count
    position = ((tm_index >> 1) & 1) * stream_count + stream_index
    moved = (position + shift) % ring
    tm_moved = (tm_index & ~2) | ((moved // stream_count) << 1)
    return tm_moved * stream_count + moved % stream_count


def ring_pull(value, shift):
    stream_count = lax.axis_size("stream")
    total = lax.axis_size("tm") * stream_count
    pairs = [(ring_source(target, shift, stream_count), target) for target in range(total)]
    return lax.ppermute(value, ("tm", "stream"), pairs)


def ring_gather(block):
    stream_count = lax.axis_size("stream")
    if stream_count != 4 or lax.axis_size("tm") % 4 or block.shape[1] % 256:
        return lax.all_gather(block, "stream", axis=0, tiled=True)
    rows, width = block.shape
    stream_index = lax.axis_index("stream")
    split = width // 2
    two_away = jnp.concatenate(
        [ring_pull(block[:, :split], 2), ring_pull(block[:, split:], -2)], axis=1
    )
    stacked = jnp.concatenate([block, ring_pull(block, 1), two_away, ring_pull(block, -1)], axis=0)
    doubled = jnp.concatenate([stacked, stacked], axis=0)
    start = ((stream_count - stream_index) % stream_count) * rows
    return lax.dynamic_slice_in_dim(doubled, start, stream_count * rows, 0)


def contract_last(left, right):
    return lax.dot_general(
        left, right, (((1,), (1,)), ((), ())), preferred_element_type=jnp.float32
    )


def contract_first(left, right):
    return lax.dot_general(
        left, right, (((0,), (0,)), ((), ())), preferred_element_type=jnp.float32
    )


def per_device(series, loss_grad, query_weight, keyval_weight, output_weight, lengths):
    record_rows = series[0]
    outer_grad = loss_grad[0]
    valid_count = lengths[0]
    shard_tokens = record_rows.shape[0]
    keyval_width = keyval_weight.shape[1]
    key_width = keyval_width // 2
    group_size = HEADS // KV_HEADS
    tile_rows = min(128, shard_tokens)
    key_span = REACH * shard_tokens + tile_rows
    score_scale = HEAD_DIM ** (-0.5)
    anchor = lax.axis_index("tm") * shard_tokens
    query_width = query_weight.shape[1]
    weights_local = jnp.concatenate([query_weight, keyval_weight, output_weight], axis=1)
    if lax.axis_size("tm") % 2 == 0 and weights_local.shape[1] % 256 == 0:
        half_width = weights_local.shape[1] // 2
        core = lax.axis_index("tm") % 2
        mine = ring_gather(lax.dynamic_slice_in_dim(weights_local, core * half_width, half_width, 1))
        other = xor_swap(mine, "tm", 0)
        weights_full = jnp.concatenate(
            [jnp.where(core == 0, mine, other), jnp.where(core == 0, other, mine)], axis=1
        )
    else:
        weights_full = lax.all_gather(weights_local, "stream", axis=0, tiled=True)
    query_full = weights_full[:, :query_width]
    keyval_full = weights_full[:, query_width : query_width + keyval_width]
    output_full = weights_full[:, query_width + keyval_width :]
    queries = jnp.dot(record_rows, query_full, preferred_element_type=jnp.float32).astype(
        jnp.bfloat16
    )
    keyvals = jnp.dot(record_rows, keyval_full, preferred_element_type=jnp.float32).astype(
        jnp.bfloat16
    )
    attn_grad = contract_last(outer_grad, output_full).astype(jnp.bfloat16)
    earlier = [shifted(keyvals, "tm", offset) for offset in range(REACH, 0, -1)]
    window_keyvals = jnp.concatenate(earlier + [keyvals], axis=0)
    key_parts = []
    value_parts = []
    query_grads = []
    for head_group in range(KV_HEADS):
        query_cols = slice(
            head_group * group_size * HEAD_DIM, (head_group + 1) * group_size * HEAD_DIM
        )
        key_cols = slice(head_group * HEAD_DIM, (head_group + 1) * HEAD_DIM)
        value_cols = slice(
            key_width + head_group * HEAD_DIM, key_width + (head_group + 1) * HEAD_DIM
        )
        group_key = None
        group_value = None
        query_tile = queries[0:tile_rows, query_cols].reshape(tile_rows, group_size, HEAD_DIM)
        key_tile = window_keyvals[0:key_span, key_cols]
        value_tile = window_keyvals[0:key_span, value_cols]
        query_pos = anchor + 0 + jnp.arange(tile_rows, dtype=jnp.int32)
        key_pos = anchor - REACH * shard_tokens + 0 + jnp.arange(key_span, dtype=jnp.int32)
        live_rows = query_pos < valid_count
        allowed = (key_pos[None, :] <= query_pos[:, None]) & (
            query_pos[:, None] - key_pos[None, :] < REACH * shard_tokens
        )
        allowed = (
            allowed
            & (key_pos[None, :] >= 0)
            & (key_pos[None, :] < valid_count)
            & live_rows[:, None]
        )
        scores = (
            jnp.einsum("qjd,kd->jqk", query_tile, key_tile, preferred_element_type=jnp.float32)
            * score_scale
        )
        masked = jnp.where(allowed, scores, -1e30)
        row_max = jnp.max(masked, axis=-1, keepdims=True)
        terms = jnp.where(allowed, jnp.exp(masked - row_max), 0.0)
        denom = jnp.sum(terms, axis=-1, keepdims=True)
        denom = jnp.where(live_rows[:, None], denom, 1.0)
        attn_probs = (terms / denom).astype(jnp.bfloat16)
        attn_tile = jnp.einsum(
            "jqk,kd->qjd", attn_probs, value_tile, preferred_element_type=jnp.float32
        ).astype(jnp.bfloat16)
        grad_tile = attn_grad[0:tile_rows, query_cols].reshape(tile_rows, group_size, HEAD_DIM)
        row_delta = jnp.sum(
            grad_tile.astype(jnp.float32) * attn_tile.astype(jnp.float32), axis=-1
        ).T[:, :, None]
        prob_grad = jnp.einsum(
            "qjd,kd->jqk", grad_tile, value_tile, preferred_element_type=jnp.float32
        )
        score_grad = (
            attn_probs.astype(jnp.float32) * (prob_grad - row_delta) * score_scale
        ).astype(jnp.bfloat16)
        query_grad = jnp.einsum(
            "jqk,kd->qjd", score_grad, key_tile, preferred_element_type=jnp.float32
        ).astype(jnp.bfloat16)
        key_grad = jnp.einsum(
            "jqk,qjd->kd", score_grad, query_tile, preferred_element_type=jnp.float32
        )
        value_grad = jnp.einsum(
            "jqk,qjd->kd", attn_probs, grad_tile, preferred_element_type=jnp.float32
        )
        group_key = key_grad
        group_value = value_grad
        tile_list = query_grad.reshape(tile_rows, group_size * HEAD_DIM)
        key_parts.append(group_key)
        value_parts.append(group_value)
        query_grads.append(tile_list)
    query_grad_all = jnp.concatenate(query_grads, axis=1)
    partial_value = jnp.concatenate(key_parts + value_parts, axis=1)

    def shard_slot(offset):
        return partial_value[(REACH - offset) * shard_tokens : (REACH - offset + 1) * shard_tokens]

    summed = shard_slot(0)
    for offset in range(1, REACH + 1):
        summed = summed + shifted(shard_slot(offset).astype(jnp.bfloat16), "tm", -offset).astype(
            jnp.float32
        )
    keyval_grads = summed.astype(jnp.bfloat16)
    input_grad = contract_last(query_grad_all, query_full) + contract_last(
        keyval_grads, keyval_full
    )
    input_grad = input_grad.astype(jnp.bfloat16)
    weight_grad = grad_sum((record_rows, keyval_grads))
    return (input_grad[None], weight_grad)


def solution(mesh):
    placed = (
        P("stream", "tm", None),
        P("stream", "tm", None),
        P("stream", None),
        P("stream", None),
        P("stream", None),
        P("stream"),
    )
    return jax.shard_map(
        per_device,
        mesh=mesh,
        in_specs=placed,
        out_specs=(P("stream", "tm", None), P("stream", None)),
        check_vma=False,
    )
```

```python
import jax
import jax.numpy as jnp
from jax import lax
from jax.sharding import PartitionSpec as P

HEADS = 16
KV_HEADS = 4
HEAD_DIM = 64
REACH = 4


def shifted(value, axis, steps):
    count = lax.axis_size(axis)
    leading, last = (max(0, -steps), min(count, count - steps))
    return lax.ppermute(value, axis, [(source, source + steps) for source in range(leading, last)])


def xor_swap(value, axis, bit):
    count = lax.axis_size(axis)
    return lax.ppermute(value, axis, [(source, source ^ (1 << bit)) for source in range(count)])


def tree_psum(value, axis):
    count = lax.axis_size(axis)
    bits = count.bit_length() - 1
    if count != 1 << bits or value.shape[0] % count:
        return lax.psum(value, axis)
    order = [b for b in (0, 2, 4, 1, 3, 5, 6) if b < bits] + list(range(7, bits))
    index = lax.axis_index(axis)
    current = value
    for bit in order:
        half = current.shape[0] // 2
        upper = ((index >> bit) & 1) == 1
        low, high = current[:half], current[half:]
        keep = jnp.where(upper, high, low)
        send = jnp.where(upper, low, high)
        current = keep + xor_swap(send, axis, bit)
    for bit in reversed(order):
        upper = ((index >> bit) & 1) == 1
        other = xor_swap(current, axis, bit)
        current = jnp.where(
            upper, jnp.concatenate([other, current]), jnp.concatenate([current, other])
        )
    return current


def halve_stage(value, axis, bit, wire):
    half = value.shape[0] // 2
    upper = ((lax.axis_index(axis) >> bit) & 1) == 1
    low, high = value[:half], value[half:]
    keep = jnp.where(upper, high, low).astype(jnp.float32)
    send = jnp.where(upper, low, high)
    return keep + xor_swap(send.astype(wire), axis, bit).astype(jnp.float32)


def double_stage(value, axis, bit):
    upper = ((lax.axis_index(axis) >> bit) & 1) == 1
    other = xor_swap(value, axis, bit)
    return jnp.where(upper, jnp.concatenate([other, value]), jnp.concatenate([value, other]))


NEAR_BITS = (2, 4)


def grad_sum(partial):
    stream_count = lax.axis_size("stream")
    tm_count = lax.axis_size("tm")
    stream_bits = stream_count.bit_length() - 1
    tm_bits = tm_count.bit_length() - 1
    rows, grads = partial
    tokens, features = rows.shape
    if (
        stream_count != 1 << stream_bits
        or tm_count != 1 << tm_bits
        or stream_bits == 0
        or tm_bits == 0
        or features % (2 * stream_count)
        or grads.shape[1] % 256
    ):
        shard = lax.psum_scatter(
            contract_first(rows, grads).astype(jnp.bfloat16), "stream", scatter_dimension=0, tiled=True
        ).astype(jnp.float32)
        return lax.psum(shard, "tm")
    stream_index = lax.axis_index("stream")
    core = lax.axis_index("tm") % 2
    half_cols = grads.shape[1] // 2
    paired = rows.reshape(tokens, stream_count // 2, 2, features // stream_count)
    even = paired[:, :, 0].reshape(tokens, features // 2)
    odd = paired[:, :, 1].reshape(tokens, features // 2)
    upper = (stream_index & 1) == 1
    ordered = jnp.concatenate([jnp.where(upper, odd, even), jnp.where(upper, even, odd)], axis=1)
    mine_cols = lax.dynamic_slice_in_dim(grads, core * half_cols, half_cols, 1)
    other_cols = lax.dynamic_slice_in_dim(grads, (1 - core) * half_cols, half_cols, 1)
    current = contract_first(ordered, mine_cols) + xor_swap(
        contract_first(ordered, other_cols), "tm", 0
    )
    half_rows = features // 2
    current = current[:half_rows] + xor_swap(
        current[half_rows:].astype(jnp.bfloat16), "stream", 0
    ).astype(jnp.float32)
    for bit in reversed(range(1, stream_bits)):
        current = halve_stage(current, "stream", bit, jnp.bfloat16)
    near = [bit for bit in NEAR_BITS if bit < tm_bits]
    near = near[: max(0, current.shape[0].bit_length() - 1)]
    for bit in near:
        current = halve_stage(current, "tm", bit, jnp.float32)
    for bit in range(1, tm_bits):
        if bit not in near:
            current = current + xor_swap(current, "tm", bit)
    for bit in reversed(near):
        current = double_stage(current, "tm", bit)
    other = xor_swap(current, "tm", 0)
    return jnp.where(
        core == 1,
        jnp.concatenate([other, current], axis=1),
        jnp.concatenate([current, other], axis=1),
    )


def ring_source(linear, shift, stream_count):
    tm_index, stream_index = divmod(linear, stream_count)
    ring = 2 * stream_count
    position = ((tm_index >> 1) & 1) * stream_count + stream_index
    moved = (position + shift) % ring
    tm_moved = (tm_index & ~2) | ((moved // stream_count) << 1)
    return tm_moved * stream_count + moved % stream_count


def ring_pull(value, shift):
    stream_count = lax.axis_size("stream")
    total = lax.axis_size("tm") * stream_count
    pairs = [(ring_source(target, shift, stream_count), target) for target in range(total)]
    return lax.ppermute(value, ("tm", "stream"), pairs)


def ring_gather(block):
    stream_count = lax.axis_size("stream")
    if stream_count != 4 or lax.axis_size("tm") % 4 or block.shape[1] % 256:
        return lax.all_gather(block, "stream", axis=0, tiled=True), 0
    rows, width = block.shape
    stream_index = lax.axis_index("stream")
    split = width // 2
    two_away = jnp.concatenate(
        [ring_pull(block[:, :split], 2), ring_pull(block[:, split:], -2)], axis=1
    )
    stacked = jnp.concatenate([block, ring_pull(block, 1), two_away, ring_pull(block, -1)], axis=0)
    return stacked, stream_index


def rotate_cols(value, blocks, shift):
    width = value.shape[1] // blocks
    doubled = jnp.concatenate([value, value], axis=1)
    return lax.dynamic_slice_in_dim(doubled, (shift % blocks) * width, value.shape[1], 1)


def contract_last(left, right):
    return lax.dot_general(
        left, right, (((1,), (1,)), ((), ())), preferred_element_type=jnp.float32
    )


def contract_first(left, right):
    return lax.dot_general(
        left, right, (((0,), (0,)), ((), ())), preferred_element_type=jnp.float32
    )


def per_device(series, loss_grad, query_weight, keyval_weight, output_weight, lengths):
    record_rows = series[0]
    outer_grad = loss_grad[0]
    valid_count = lengths[0]
    shard_tokens = record_rows.shape[0]
    keyval_width = keyval_weight.shape[1]
    key_width = keyval_width // 2
    group_size = HEADS // KV_HEADS
    tile_rows = min(128, shard_tokens)
    key_span = REACH * shard_tokens + tile_rows
    score_scale = HEAD_DIM ** (-0.5)
    anchor = lax.axis_index("tm") * shard_tokens
    query_width = query_weight.shape[1]
    weights_local = jnp.concatenate([query_weight, keyval_weight, output_weight], axis=1)
    if lax.axis_size("tm") % 2 == 0 and weights_local.shape[1] % 256 == 0:
        half_width = weights_local.shape[1] // 2
        core = lax.axis_index("tm") % 2
        mine, rotation = ring_gather(
            lax.dynamic_slice_in_dim(weights_local, core * half_width, half_width, 1)
        )
        other = xor_swap(mine, "tm", 0)
        weights_full = jnp.concatenate(
            [jnp.where(core == 0, mine, other), jnp.where(core == 0, other, mine)], axis=1
        )
    else:
        weights_full = lax.all_gather(weights_local, "stream", axis=0, tiled=True)
        rotation = 0
    stream_count = lax.axis_size("stream")
    rotated_rows = rotate_cols(record_rows, stream_count, rotation)
    query_full = weights_full[:, :query_width]
    keyval_full = weights_full[:, query_width : query_width + keyval_width]
    output_full = weights_full[:, query_width + keyval_width :]
    queries = jnp.dot(rotated_rows, query_full, preferred_element_type=jnp.float32).astype(
        jnp.bfloat16
    )
    keyvals = jnp.dot(rotated_rows, keyval_full, preferred_element_type=jnp.float32).astype(
        jnp.bfloat16
    )
    attn_grad = rotate_cols(
        contract_last(outer_grad, output_full).astype(jnp.bfloat16), stream_count, -rotation
    )
    earlier = [shifted(keyvals, "tm", offset) for offset in range(REACH, 0, -1)]
    window_keyvals = jnp.concatenate(earlier + [keyvals], axis=0)
    key_parts = []
    value_parts = []
    query_grads = []
    for head_group in range(KV_HEADS):
        query_cols = slice(
            head_group * group_size * HEAD_DIM, (head_group + 1) * group_size * HEAD_DIM
        )
        key_cols = slice(head_group * HEAD_DIM, (head_group + 1) * HEAD_DIM)
        value_cols = slice(
            key_width + head_group * HEAD_DIM, key_width + (head_group + 1) * HEAD_DIM
        )
        group_key = None
        group_value = None
        query_tile = queries[0:tile_rows, query_cols].reshape(tile_rows, group_size, HEAD_DIM)
        key_tile = window_keyvals[0:key_span, key_cols]
        value_tile = window_keyvals[0:key_span, value_cols]
        query_pos = anchor + 0 + jnp.arange(tile_rows, dtype=jnp.int32)
        key_pos = anchor - REACH * shard_tokens + 0 + jnp.arange(key_span, dtype=jnp.int32)
        live_rows = query_pos < valid_count
        allowed = (key_pos[None, :] <= query_pos[:, None]) & (
            query_pos[:, None] - key_pos[None, :] < REACH * shard_tokens
        )
        allowed = (
            allowed
            & (key_pos[None, :] >= 0)
            & (key_pos[None, :] < valid_count)
            & live_rows[:, None]
        )
        scores = (
            jnp.einsum("qjd,kd->jqk", query_tile, key_tile, preferred_element_type=jnp.float32)
            * score_scale
        )
        masked = jnp.where(allowed, scores, -1e30)
        row_max = jnp.max(masked, axis=-1, keepdims=True)
        terms = jnp.where(allowed, jnp.exp(masked - row_max), 0.0)
        denom = jnp.sum(terms, axis=-1, keepdims=True)
        denom = jnp.where(live_rows[:, None], denom, 1.0)
        attn_probs = (terms / denom).astype(jnp.bfloat16)
        attn_tile = jnp.einsum(
            "jqk,kd->qjd", attn_probs, value_tile, preferred_element_type=jnp.float32
        ).astype(jnp.bfloat16)
        grad_tile = attn_grad[0:tile_rows, query_cols].reshape(tile_rows, group_size, HEAD_DIM)
        row_delta = jnp.sum(
            grad_tile.astype(jnp.float32) * attn_tile.astype(jnp.float32), axis=-1
        ).T[:, :, None]
        prob_grad = jnp.einsum(
            "qjd,kd->jqk", grad_tile, value_tile, preferred_element_type=jnp.float32
        )
        score_grad = (
            attn_probs.astype(jnp.float32) * (prob_grad - row_delta) * score_scale
        ).astype(jnp.bfloat16)
        query_grad = jnp.einsum(
            "jqk,kd->qjd", score_grad, key_tile, preferred_element_type=jnp.float32
        ).astype(jnp.bfloat16)
        key_grad = jnp.einsum(
            "jqk,qjd->kd", score_grad, query_tile, preferred_element_type=jnp.float32
        )
        value_grad = jnp.einsum(
            "jqk,qjd->kd", attn_probs, grad_tile, preferred_element_type=jnp.float32
        )
        group_key = key_grad
        group_value = value_grad
        tile_list = query_grad.reshape(tile_rows, group_size * HEAD_DIM)
        key_parts.append(group_key)
        value_parts.append(group_value)
        query_grads.append(tile_list)
    query_grad_all = jnp.concatenate(query_grads, axis=1)
    partial_value = jnp.concatenate(key_parts + value_parts, axis=1)

    def shard_slot(offset):
        return partial_value[(REACH - offset) * shard_tokens : (REACH - offset + 1) * shard_tokens]

    summed = shard_slot(0)
    for offset in range(1, REACH + 1):
        summed = summed + shifted(shard_slot(offset).astype(jnp.bfloat16), "tm", -offset).astype(
            jnp.float32
        )
    keyval_grads = summed.astype(jnp.bfloat16)
    input_grad = contract_last(query_grad_all, query_full) + contract_last(
        keyval_grads, keyval_full
    )
    input_grad = rotate_cols(input_grad.astype(jnp.bfloat16), stream_count, -rotation)
    weight_grad = grad_sum((record_rows, keyval_grads))
    return (input_grad[None], weight_grad)


def solution(mesh):
    placed = (
        P("stream", "tm", None),
        P("stream", "tm", None),
        P("stream", None),
        P("stream", None),
        P("stream", None),
        P("stream"),
    )
    return jax.shard_map(
        per_device,
        mesh=mesh,
        in_specs=placed,
        out_specs=(P("stream", "tm", None), P("stream", None)),
        check_vma=False,
    )
```

```python
import jax
import jax.numpy as jnp
from jax import lax
from jax.sharding import PartitionSpec as P

HEADS = 16
KV_HEADS = 4
HEAD_DIM = 64
REACH = 4


def shifted(value, axis, steps):
    count = lax.axis_size(axis)
    leading, last = (max(0, -steps), min(count, count - steps))
    return lax.ppermute(value, axis, [(source, source + steps) for source in range(leading, last)])


def xor_swap(value, axis, bit):
    count = lax.axis_size(axis)
    return lax.ppermute(value, axis, [(source, source ^ (1 << bit)) for source in range(count)])


def tree_psum(value, axis):
    count = lax.axis_size(axis)
    bits = count.bit_length() - 1
    if count != 1 << bits or value.shape[0] % count:
        return lax.psum(value, axis)
    order = [b for b in (0, 2, 4, 1, 3, 5, 6) if b < bits] + list(range(7, bits))
    index = lax.axis_index(axis)
    current = value
    for bit in order:
        half = current.shape[0] // 2
        upper = ((index >> bit) & 1) == 1
        low, high = current[:half], current[half:]
        keep = jnp.where(upper, high, low)
        send = jnp.where(upper, low, high)
        current = keep + xor_swap(send, axis, bit)
    for bit in reversed(order):
        upper = ((index >> bit) & 1) == 1
        other = xor_swap(current, axis, bit)
        current = jnp.where(
            upper, jnp.concatenate([other, current]), jnp.concatenate([current, other])
        )
    return current


def halve_stage(value, axis, bit, wire):
    half = value.shape[0] // 2
    upper = ((lax.axis_index(axis) >> bit) & 1) == 1
    low, high = value[:half], value[half:]
    keep = jnp.where(upper, high, low).astype(jnp.float32)
    send = jnp.where(upper, low, high)
    return keep + xor_swap(send.astype(wire), axis, bit).astype(jnp.float32)


def double_stage(value, axis, bit):
    upper = ((lax.axis_index(axis) >> bit) & 1) == 1
    other = xor_swap(value, axis, bit)
    return jnp.where(upper, jnp.concatenate([other, value]), jnp.concatenate([value, other]))


NEAR_BITS = (2, 4)


def grad_sum(partial):
    stream_count = lax.axis_size("stream")
    tm_count = lax.axis_size("tm")
    stream_bits = stream_count.bit_length() - 1
    tm_bits = tm_count.bit_length() - 1
    rows, grads = partial
    tokens, features = rows.shape
    if (
        stream_count != 1 << stream_bits
        or tm_count != 1 << tm_bits
        or stream_bits == 0
        or tm_bits == 0
        or features % (2 * stream_count)
        or grads.shape[1] % 256
    ):
        shard = lax.psum_scatter(
            contract_first(rows, grads).astype(jnp.bfloat16), "stream", scatter_dimension=0, tiled=True
        ).astype(jnp.float32)
        return lax.psum(shard, "tm")
    stream_index = lax.axis_index("stream")
    core = lax.axis_index("tm") % 2
    half_cols = grads.shape[1] // 2
    paired = rows.reshape(tokens, stream_count // 2, 2, features // stream_count)
    even = paired[:, :, 0].reshape(tokens, features // 2)
    odd = paired[:, :, 1].reshape(tokens, features // 2)
    upper = (stream_index & 1) == 1
    ordered = jnp.concatenate([jnp.where(upper, odd, even), jnp.where(upper, even, odd)], axis=1)
    mine_cols = lax.dynamic_slice_in_dim(grads, core * half_cols, half_cols, 1)
    other_cols = lax.dynamic_slice_in_dim(grads, (1 - core) * half_cols, half_cols, 1)
    current = contract_first(ordered, mine_cols) + xor_swap(
        contract_first(ordered, other_cols), "tm", 0
    )
    half_rows = features // 2
    current = current[:half_rows] + xor_swap(
        current[half_rows:].astype(jnp.bfloat16), "stream", 0
    ).astype(jnp.float32)
    for bit in reversed(range(1, stream_bits)):
        current = halve_stage(current, "stream", bit, jnp.bfloat16)
    near = [bit for bit in NEAR_BITS if bit < tm_bits]
    near = near[: max(0, current.shape[0].bit_length() - 1)]
    for bit in near:
        current = halve_stage(current, "tm", bit, jnp.float32)
    for bit in range(1, tm_bits):
        if bit not in near:
            current = current + xor_swap(current, "tm", bit)
    for bit in reversed(near):
        current = double_stage(current, "tm", bit)
    other = xor_swap(current, "tm", 0)
    return jnp.where(
        core == 1,
        jnp.concatenate([other, current], axis=1),
        jnp.concatenate([current, other], axis=1),
    )


def ring_source(linear, shift, stream_count):
    tm_index, stream_index = divmod(linear, stream_count)
    ring = 2 * stream_count
    position = ((tm_index >> 1) & 1) * stream_count + stream_index
    moved = (position + shift) % ring
    tm_moved = (tm_index & ~2) | ((moved // stream_count) << 1)
    return tm_moved * stream_count + moved % stream_count


def ring_pull(value, shift):
    stream_count = lax.axis_size("stream")
    total = lax.axis_size("tm") * stream_count
    pairs = [(ring_source(target, shift, stream_count), target) for target in range(total)]
    return lax.ppermute(value, ("tm", "stream"), pairs)


def ring_gather(block):
    stream_count = lax.axis_size("stream")
    if stream_count != 4 or lax.axis_size("tm") % 4 or block.shape[1] % 256:
        return lax.all_gather(block, "stream", axis=0, tiled=True)
    rows, width = block.shape
    stream_index = lax.axis_index("stream")
    split = width // 2
    two_away = jnp.concatenate(
        [ring_pull(block[:, :split], 2), ring_pull(block[:, split:], -2)], axis=1
    )
    arrived = [block, ring_pull(block, 1), two_away, ring_pull(block, -1)]
    placed = []
    for position in range(stream_count):
        offset = (position - stream_index) % stream_count
        chosen = arrived[3]
        for slot in (2, 1, 0):
            chosen = jnp.where(offset == slot, arrived[slot], chosen)
        placed.append(chosen)
    return jnp.concatenate(placed, axis=0)


def contract_last(left, right):
    return lax.dot_general(
        left, right, (((1,), (1,)), ((), ())), preferred_element_type=jnp.float32
    )


def contract_first(left, right):
    return lax.dot_general(
        left, right, (((0,), (0,)), ((), ())), preferred_element_type=jnp.float32
    )


def per_device(series, loss_grad, query_weight, keyval_weight, output_weight, lengths):
    record_rows = series[0]
    outer_grad = loss_grad[0]
    valid_count = lengths[0]
    shard_tokens = record_rows.shape[0]
    keyval_width = keyval_weight.shape[1]
    key_width = keyval_width // 2
    group_size = HEADS // KV_HEADS
    tile_rows = min(128, shard_tokens)
    key_span = REACH * shard_tokens + tile_rows
    score_scale = HEAD_DIM ** (-0.5)
    anchor = lax.axis_index("tm") * shard_tokens
    query_width = query_weight.shape[1]
    weights_local = jnp.concatenate([query_weight, keyval_weight, output_weight], axis=1)
    if lax.axis_size("tm") % 2 == 0 and weights_local.shape[1] % 256 == 0:
        half_width = weights_local.shape[1] // 2
        core = lax.axis_index("tm") % 2
        mine = ring_gather(lax.dynamic_slice_in_dim(weights_local, core * half_width, half_width, 1))
        other = xor_swap(mine, "tm", 0)
        weights_full = jnp.concatenate(
            [jnp.where(core == 0, mine, other), jnp.where(core == 0, other, mine)], axis=1
        )
    else:
        weights_full = lax.all_gather(weights_local, "stream", axis=0, tiled=True)
    query_full = weights_full[:, :query_width]
    keyval_full = weights_full[:, query_width : query_width + keyval_width]
    output_full = weights_full[:, query_width + keyval_width :]
    queries = jnp.dot(record_rows, query_full, preferred_element_type=jnp.float32).astype(
        jnp.bfloat16
    )
    keyvals = jnp.dot(record_rows, keyval_full, preferred_element_type=jnp.float32).astype(
        jnp.bfloat16
    )
    attn_grad = contract_last(outer_grad, output_full).astype(jnp.bfloat16)
    earlier = [shifted(keyvals, "tm", offset) for offset in range(REACH, 0, -1)]
    window_keyvals = jnp.concatenate(earlier + [keyvals], axis=0)
    key_parts = []
    value_parts = []
    query_grads = []
    for head_group in range(KV_HEADS):
        query_cols = slice(
            head_group * group_size * HEAD_DIM, (head_group + 1) * group_size * HEAD_DIM
        )
        key_cols = slice(head_group * HEAD_DIM, (head_group + 1) * HEAD_DIM)
        value_cols = slice(
            key_width + head_group * HEAD_DIM, key_width + (head_group + 1) * HEAD_DIM
        )
        group_key = None
        group_value = None
        query_tile = queries[0:tile_rows, query_cols].reshape(tile_rows, group_size, HEAD_DIM)
        key_tile = window_keyvals[0:key_span, key_cols]
        value_tile = window_keyvals[0:key_span, value_cols]
        query_pos = anchor + 0 + jnp.arange(tile_rows, dtype=jnp.int32)
        key_pos = anchor - REACH * shard_tokens + 0 + jnp.arange(key_span, dtype=jnp.int32)
        live_rows = query_pos < valid_count
        allowed = (key_pos[None, :] <= query_pos[:, None]) & (
            query_pos[:, None] - key_pos[None, :] < REACH * shard_tokens
        )
        allowed = (
            allowed
            & (key_pos[None, :] >= 0)
            & (key_pos[None, :] < valid_count)
            & live_rows[:, None]
        )
        scores = (
            jnp.einsum("qjd,kd->jqk", query_tile, key_tile, preferred_element_type=jnp.float32)
            * score_scale
        )
        masked = jnp.where(allowed, scores, -1e30)
        row_max = jnp.max(masked, axis=-1, keepdims=True)
        terms = jnp.where(allowed, jnp.exp(masked - row_max), 0.0)
        denom = jnp.sum(terms, axis=-1, keepdims=True)
        denom = jnp.where(live_rows[:, None], denom, 1.0)
        attn_probs = (terms / denom).astype(jnp.bfloat16)
        attn_tile = jnp.einsum(
            "jqk,kd->qjd", attn_probs, value_tile, preferred_element_type=jnp.float32
        ).astype(jnp.bfloat16)
        grad_tile = attn_grad[0:tile_rows, query_cols].reshape(tile_rows, group_size, HEAD_DIM)
        row_delta = jnp.sum(
            grad_tile.astype(jnp.float32) * attn_tile.astype(jnp.float32), axis=-1
        ).T[:, :, None]
        prob_grad = jnp.einsum(
            "qjd,kd->jqk", grad_tile, value_tile, preferred_element_type=jnp.float32
        )
        score_grad = (
            attn_probs.astype(jnp.float32) * (prob_grad - row_delta) * score_scale
        ).astype(jnp.bfloat16)
        query_grad = jnp.einsum(
            "jqk,kd->qjd", score_grad, key_tile, preferred_element_type=jnp.float32
        ).astype(jnp.bfloat16)
        key_grad = jnp.einsum(
            "jqk,qjd->kd", score_grad, query_tile, preferred_element_type=jnp.float32
        )
        value_grad = jnp.einsum(
            "jqk,qjd->kd", attn_probs, grad_tile, preferred_element_type=jnp.float32
        )
        group_key = key_grad
        group_value = value_grad
        tile_list = query_grad.reshape(tile_rows, group_size * HEAD_DIM)
        key_parts.append(group_key)
        value_parts.append(group_value)
        query_grads.append(tile_list)
    query_grad_all = jnp.concatenate(query_grads, axis=1)
    partial_value = jnp.concatenate(key_parts + value_parts, axis=1)

    def shard_slot(offset):
        return partial_value[(REACH - offset) * shard_tokens : (REACH - offset + 1) * shard_tokens]

    summed = shard_slot(0)
    for offset in range(1, REACH + 1):
        summed = summed + shifted(shard_slot(offset).astype(jnp.bfloat16), "tm", -offset).astype(
            jnp.float32
        )
    keyval_grads = summed.astype(jnp.bfloat16)
    input_grad = contract_last(query_grad_all, query_full) + contract_last(
        keyval_grads, keyval_full
    )
    input_grad = input_grad.astype(jnp.bfloat16)
    weight_grad = grad_sum((record_rows, keyval_grads))
    return (input_grad[None], weight_grad)


def solution(mesh):
    placed = (
        P("stream", "tm", None),
        P("stream", "tm", None),
        P("stream", None),
        P("stream", None),
        P("stream", None),
        P("stream"),
    )
    return jax.shard_map(
        per_device,
        mesh=mesh,
        in_specs=placed,
        out_specs=(P("stream", "tm", None), P("stream", None)),
        check_vma=False,
    )
```

```python
import jax
import jax.numpy as jnp
from jax import lax
from jax.sharding import PartitionSpec as P

HEADS = 16
KV_HEADS = 4
HEAD_DIM = 64
REACH = 4


def shifted(value, axis, steps):
    count = lax.axis_size(axis)
    leading, last = (max(0, -steps), min(count, count - steps))
    return lax.ppermute(value, axis, [(source, source + steps) for source in range(leading, last)])


def xor_swap(value, axis, bit):
    count = lax.axis_size(axis)
    return lax.ppermute(value, axis, [(source, source ^ (1 << bit)) for source in range(count)])


def tree_psum(value, axis):
    count = lax.axis_size(axis)
    bits = count.bit_length() - 1
    if count != 1 << bits or value.shape[0] % count:
        return lax.psum(value, axis)
    order = [b for b in (0, 2, 4, 1, 3, 5, 6) if b < bits] + list(range(7, bits))
    index = lax.axis_index(axis)
    current = value
    for bit in order:
        half = current.shape[0] // 2
        upper = ((index >> bit) & 1) == 1
        low, high = current[:half], current[half:]
        keep = jnp.where(upper, high, low)
        send = jnp.where(upper, low, high)
        current = keep + xor_swap(send, axis, bit)
    for bit in reversed(order):
        upper = ((index >> bit) & 1) == 1
        other = xor_swap(current, axis, bit)
        current = jnp.where(
            upper, jnp.concatenate([other, current]), jnp.concatenate([current, other])
        )
    return current


def halve_stage(value, axis, bit, wire):
    half = value.shape[0] // 2
    upper = ((lax.axis_index(axis) >> bit) & 1) == 1
    low, high = value[:half], value[half:]
    keep = jnp.where(upper, high, low).astype(jnp.float32)
    send = jnp.where(upper, low, high)
    return keep + xor_swap(send.astype(wire), axis, bit).astype(jnp.float32)


def double_stage(value, axis, bit):
    upper = ((lax.axis_index(axis) >> bit) & 1) == 1
    other = xor_swap(value, axis, bit)
    return jnp.where(upper, jnp.concatenate([other, value]), jnp.concatenate([value, other]))


NEAR_BITS = (2, 4)


def grad_sum(partial):
    stream_count = lax.axis_size("stream")
    tm_count = lax.axis_size("tm")
    stream_bits = stream_count.bit_length() - 1
    tm_bits = tm_count.bit_length() - 1
    rows, grads = partial
    tokens, features = rows.shape
    if (
        stream_count != 1 << stream_bits
        or tm_count != 1 << tm_bits
        or stream_bits == 0
        or tm_bits == 0
        or features % (2 * stream_count)
        or grads.shape[1] % 256
    ):
        shard = lax.psum_scatter(
            contract_first(rows, grads).astype(jnp.bfloat16), "stream", scatter_dimension=0, tiled=True
        ).astype(jnp.float32)
        return lax.psum(shard, "tm")
    stream_index = lax.axis_index("stream")
    core = lax.axis_index("tm") % 2
    half_cols = grads.shape[1] // 2
    paired = rows.reshape(tokens, stream_count // 2, 2, features // stream_count)
    even = paired[:, :, 0].reshape(tokens, features // 2)
    odd = paired[:, :, 1].reshape(tokens, features // 2)
    upper = (stream_index & 1) == 1
    ordered = jnp.concatenate([jnp.where(upper, odd, even), jnp.where(upper, even, odd)], axis=1)
    mine_cols = lax.dynamic_slice_in_dim(grads, core * half_cols, half_cols, 1)
    other_cols = lax.dynamic_slice_in_dim(grads, (1 - core) * half_cols, half_cols, 1)
    current = contract_first(ordered, mine_cols) + xor_swap(
        contract_first(ordered, other_cols), "tm", 0
    )
    half_rows = features // 2
    current = current[:half_rows] + xor_swap(
        current[half_rows:].astype(jnp.bfloat16), "stream", 0
    ).astype(jnp.float32)
    for bit in reversed(range(1, stream_bits)):
        current = halve_stage(current, "stream", bit, jnp.bfloat16)
    near = [bit for bit in NEAR_BITS if bit < tm_bits]
    near = near[: max(0, current.shape[0].bit_length() - 1)]
    for bit in near:
        current = halve_stage(current, "tm", bit, jnp.float32)
    for bit in range(1, tm_bits):
        if bit not in near:
            current = current + xor_swap(current, "tm", bit)
    for bit in reversed(near):
        current = double_stage(current, "tm", bit)
    other = xor_swap(current, "tm", 0)
    return jnp.where(
        core == 1,
        jnp.concatenate([other, current], axis=1),
        jnp.concatenate([current, other], axis=1),
    )


def ring_source(linear, shift, stream_count):
    tm_index, stream_index = divmod(linear, stream_count)
    ring = 2 * stream_count
    position = ((tm_index >> 1) & 1) * stream_count + stream_index
    moved = (position + shift) % ring
    tm_moved = (tm_index & ~2) | ((moved // stream_count) << 1)
    return tm_moved * stream_count + moved % stream_count


def ring_pull(value, shift):
    stream_count = lax.axis_size("stream")
    total = lax.axis_size("tm") * stream_count
    pairs = [(ring_source(target, shift, stream_count), target) for target in range(total)]
    return lax.ppermute(value, ("tm", "stream"), pairs)


def ring_gather(block):
    stream_count = lax.axis_size("stream")
    if stream_count != 4 or lax.axis_size("tm") % 4 or block.shape[1] % 256:
        return lax.all_gather(block, "stream", axis=0, tiled=True)
    rows, width = block.shape
    stream_index = lax.axis_index("stream")
    split = width // 2
    two_away = jnp.concatenate(
        [ring_pull(block[:, :split], 2), ring_pull(block[:, split:], -2)], axis=1
    )
    arrived = [block, ring_pull(block, 1), two_away, ring_pull(block, -1)]
    placed = []
    for position in range(stream_count):
        offset = (position - stream_index) % stream_count
        chosen = arrived[3]
        for slot in (2, 1, 0):
            chosen = jnp.where(offset == slot, arrived[slot], chosen)
        placed.append(chosen)
    return jnp.concatenate(placed, axis=0)


def contract_last(left, right):
    return lax.dot_general(
        left, right, (((1,), (1,)), ((), ())), preferred_element_type=jnp.float32
    )


def contract_first(left, right):
    return lax.dot_general(
        left, right, (((0,), (0,)), ((), ())), preferred_element_type=jnp.float32
    )


def per_device(series, loss_grad, query_weight, keyval_weight, output_weight, lengths):
    record_rows = series[0]
    outer_grad = loss_grad[0]
    valid_count = lengths[0]
    shard_tokens = record_rows.shape[0]
    keyval_width = keyval_weight.shape[1]
    key_width = keyval_width // 2
    group_size = HEADS // KV_HEADS
    tile_rows = min(128, shard_tokens)
    key_span = REACH * shard_tokens + tile_rows
    score_scale = HEAD_DIM ** (-0.5)
    anchor = lax.axis_index("tm") * shard_tokens
    query_width = query_weight.shape[1]
    weights_local = jnp.concatenate([query_weight, keyval_weight, output_weight], axis=1)
    if lax.axis_size("tm") % 2 == 0 and weights_local.shape[1] % 256 == 0:
        half_width = weights_local.shape[1] // 2
        core = lax.axis_index("tm") % 2
        mine = ring_gather(lax.dynamic_slice_in_dim(weights_local, core * half_width, half_width, 1))
        other = xor_swap(mine, "tm", 0)
        weights_full = jnp.concatenate(
            [jnp.where(core == 0, mine, other), jnp.where(core == 0, other, mine)], axis=1
        )
    else:
        weights_full = lax.all_gather(weights_local, "stream", axis=0, tiled=True)
    query_full = weights_full[:, :query_width]
    keyval_full = weights_full[:, query_width : query_width + keyval_width]
    output_full = weights_full[:, query_width + keyval_width :]
    queries = jnp.dot(record_rows, query_full, preferred_element_type=jnp.float32).astype(
        jnp.bfloat16
    )
    keyvals = jnp.dot(record_rows, keyval_full, preferred_element_type=jnp.float32).astype(
        jnp.bfloat16
    )
    attn_grad = contract_last(outer_grad, output_full).astype(jnp.bfloat16)
    if REACH == 4:
        back_one = shifted(keyvals, "tm", 1)
        back_pair = shifted(jnp.concatenate([back_one, keyvals], axis=0), "tm", 2)
        back_four = shifted(keyvals, "tm", 4)
        window_keyvals = jnp.concatenate([back_four, back_pair, back_one, keyvals], axis=0)
    else:
        earlier = [shifted(keyvals, "tm", offset) for offset in range(REACH, 0, -1)]
        window_keyvals = jnp.concatenate(earlier + [keyvals], axis=0)
    key_parts = []
    value_parts = []
    query_grads = []
    for head_group in range(KV_HEADS):
        query_cols = slice(
            head_group * group_size * HEAD_DIM, (head_group + 1) * group_size * HEAD_DIM
        )
        key_cols = slice(head_group * HEAD_DIM, (head_group + 1) * HEAD_DIM)
        value_cols = slice(
            key_width + head_group * HEAD_DIM, key_width + (head_group + 1) * HEAD_DIM
        )
        group_key = None
        group_value = None
        query_tile = queries[0:tile_rows, query_cols].reshape(tile_rows, group_size, HEAD_DIM)
        key_tile = window_keyvals[0:key_span, key_cols]
        value_tile = window_keyvals[0:key_span, value_cols]
        query_pos = anchor + 0 + jnp.arange(tile_rows, dtype=jnp.int32)
        key_pos = anchor - REACH * shard_tokens + 0 + jnp.arange(key_span, dtype=jnp.int32)
        live_rows = query_pos < valid_count
        allowed = (key_pos[None, :] <= query_pos[:, None]) & (
            query_pos[:, None] - key_pos[None, :] < REACH * shard_tokens
        )
        allowed = (
            allowed
            & (key_pos[None, :] >= 0)
            & (key_pos[None, :] < valid_count)
            & live_rows[:, None]
        )
        scores = (
            jnp.einsum("qjd,kd->jqk", query_tile, key_tile, preferred_element_type=jnp.float32)
            * score_scale
        )
        masked = jnp.where(allowed, scores, -1e30)
        row_max = jnp.max(masked, axis=-1, keepdims=True)
        terms = jnp.where(allowed, jnp.exp(masked - row_max), 0.0)
        denom = jnp.sum(terms, axis=-1, keepdims=True)
        denom = jnp.where(live_rows[:, None], denom, 1.0)
        attn_probs = (terms / denom).astype(jnp.bfloat16)
        attn_tile = jnp.einsum(
            "jqk,kd->qjd", attn_probs, value_tile, preferred_element_type=jnp.float32
        ).astype(jnp.bfloat16)
        grad_tile = attn_grad[0:tile_rows, query_cols].reshape(tile_rows, group_size, HEAD_DIM)
        row_delta = jnp.sum(
            grad_tile.astype(jnp.float32) * attn_tile.astype(jnp.float32), axis=-1
        ).T[:, :, None]
        prob_grad = jnp.einsum(
            "qjd,kd->jqk", grad_tile, value_tile, preferred_element_type=jnp.float32
        )
        score_grad = (
            attn_probs.astype(jnp.float32) * (prob_grad - row_delta) * score_scale
        ).astype(jnp.bfloat16)
        query_grad = jnp.einsum(
            "jqk,kd->qjd", score_grad, key_tile, preferred_element_type=jnp.float32
        ).astype(jnp.bfloat16)
        key_grad = jnp.einsum(
            "jqk,qjd->kd", score_grad, query_tile, preferred_element_type=jnp.float32
        )
        value_grad = jnp.einsum(
            "jqk,qjd->kd", attn_probs, grad_tile, preferred_element_type=jnp.float32
        )
        group_key = key_grad
        group_value = value_grad
        tile_list = query_grad.reshape(tile_rows, group_size * HEAD_DIM)
        key_parts.append(group_key)
        value_parts.append(group_value)
        query_grads.append(tile_list)
    query_grad_all = jnp.concatenate(query_grads, axis=1)
    partial_value = jnp.concatenate(key_parts + value_parts, axis=1)

    def shard_slot(offset):
        return partial_value[(REACH - offset) * shard_tokens : (REACH - offset + 1) * shard_tokens]

    if REACH == 4:
        pair_rows = jnp.concatenate([shard_slot(3), shard_slot(2)], axis=0)
        from_pair = shifted(pair_rows.astype(jnp.bfloat16), "tm", -2).astype(jnp.float32)
        from_four = shifted(shard_slot(4).astype(jnp.bfloat16), "tm", -4).astype(jnp.float32)
        slot_one = shard_slot(1) + from_pair[:shard_tokens]
        summed = shard_slot(0) + from_pair[shard_tokens:] + from_four
        summed = summed + shifted(slot_one, "tm", -1)
    else:
        summed = shard_slot(0)
        for offset in range(1, REACH + 1):
            summed = summed + shifted(
                shard_slot(offset).astype(jnp.bfloat16), "tm", -offset
            ).astype(jnp.float32)
    keyval_grads = summed.astype(jnp.bfloat16)
    input_grad = contract_last(query_grad_all, query_full) + contract_last(
        keyval_grads, keyval_full
    )
    input_grad = input_grad.astype(jnp.bfloat16)
    weight_grad = grad_sum((record_rows, keyval_grads))
    return (input_grad[None], weight_grad)


def solution(mesh):
    placed = (
        P("stream", "tm", None),
        P("stream", "tm", None),
        P("stream", None),
        P("stream", None),
        P("stream", None),
        P("stream"),
    )
    return jax.shard_map(
        per_device,
        mesh=mesh,
        in_specs=placed,
        out_specs=(P("stream", "tm", None), P("stream", None)),
        check_vma=False,
    )
```

```python
import jax
import jax.numpy as jnp
from jax import lax
from jax.sharding import PartitionSpec as P

HEADS = 16
KV_HEADS = 4
HEAD_DIM = 64
REACH = 4


def shifted(value, axis, steps):
    count = lax.axis_size(axis)
    leading, last = (max(0, -steps), min(count, count - steps))
    return lax.ppermute(value, axis, [(source, source + steps) for source in range(leading, last)])


def xor_swap(value, axis, bit):
    count = lax.axis_size(axis)
    return lax.ppermute(value, axis, [(source, source ^ (1 << bit)) for source in range(count)])


def tree_psum(value, axis):
    count = lax.axis_size(axis)
    bits = count.bit_length() - 1
    if count != 1 << bits or value.shape[0] % count:
        return lax.psum(value, axis)
    order = [b for b in (0, 2, 4, 1, 3, 5, 6) if b < bits] + list(range(7, bits))
    index = lax.axis_index(axis)
    current = value
    for bit in order:
        half = current.shape[0] // 2
        upper = ((index >> bit) & 1) == 1
        low, high = current[:half], current[half:]
        keep = jnp.where(upper, high, low)
        send = jnp.where(upper, low, high)
        current = keep + xor_swap(send, axis, bit)
    for bit in reversed(order):
        upper = ((index >> bit) & 1) == 1
        other = xor_swap(current, axis, bit)
        current = jnp.where(
            upper, jnp.concatenate([other, current]), jnp.concatenate([current, other])
        )
    return current


def halve_stage(value, axis, bit, wire):
    half = value.shape[0] // 2
    upper = ((lax.axis_index(axis) >> bit) & 1) == 1
    low, high = value[:half], value[half:]
    keep = jnp.where(upper, high, low).astype(jnp.float32)
    send = jnp.where(upper, low, high)
    return keep + xor_swap(send.astype(wire), axis, bit).astype(jnp.float32)


def double_stage(value, axis, bit):
    upper = ((lax.axis_index(axis) >> bit) & 1) == 1
    other = xor_swap(value, axis, bit)
    return jnp.where(upper, jnp.concatenate([other, value]), jnp.concatenate([value, other]))


NEAR_BITS = (2, 4)


def grad_sum(partial):
    stream_count = lax.axis_size("stream")
    tm_count = lax.axis_size("tm")
    stream_bits = stream_count.bit_length() - 1
    tm_bits = tm_count.bit_length() - 1
    rows, grads = partial
    tokens, features = rows.shape
    if (
        stream_count != 1 << stream_bits
        or tm_count != 1 << tm_bits
        or stream_bits == 0
        or tm_bits == 0
        or features % (2 * stream_count)
        or grads.shape[1] % 256
    ):
        shard = lax.psum_scatter(
            contract_first(rows, grads).astype(jnp.bfloat16), "stream", scatter_dimension=0, tiled=True
        ).astype(jnp.float32)
        return lax.psum(shard, "tm")
    stream_index = lax.axis_index("stream")
    core = lax.axis_index("tm") % 2
    half_cols = grads.shape[1] // 2
    paired = rows.reshape(tokens, stream_count // 2, 2, features // stream_count)
    even = paired[:, :, 0].reshape(tokens, features // 2)
    odd = paired[:, :, 1].reshape(tokens, features // 2)
    upper = (stream_index & 1) == 1
    ordered = jnp.concatenate([jnp.where(upper, odd, even), jnp.where(upper, even, odd)], axis=1)
    mine_cols = lax.dynamic_slice_in_dim(grads, core * half_cols, half_cols, 1)
    other_cols = lax.dynamic_slice_in_dim(grads, (1 - core) * half_cols, half_cols, 1)
    current = contract_first(ordered, mine_cols) + xor_swap(
        contract_first(ordered, other_cols).astype(jnp.bfloat16), "tm", 0
    ).astype(jnp.float32)
    half_rows = features // 2
    current = current[:half_rows] + xor_swap(
        current[half_rows:].astype(jnp.bfloat16), "stream", 0
    ).astype(jnp.float32)
    for bit in reversed(range(1, stream_bits)):
        current = halve_stage(current, "stream", bit, jnp.bfloat16)
    near = [bit for bit in NEAR_BITS if bit < tm_bits]
    near = near[: max(0, current.shape[0].bit_length() - 1)]
    for bit in near:
        current = halve_stage(current, "tm", bit, jnp.float32)
    for bit in range(1, tm_bits):
        if bit not in near:
            current = current + xor_swap(current, "tm", bit)
    for bit in reversed(near):
        current = double_stage(current, "tm", bit)
    other = xor_swap(current, "tm", 0)
    return jnp.where(
        core == 1,
        jnp.concatenate([other, current], axis=1),
        jnp.concatenate([current, other], axis=1),
    )


def ring_source(linear, shift, stream_count):
    tm_index, stream_index = divmod(linear, stream_count)
    ring = 2 * stream_count
    position = ((tm_index >> 1) & 1) * stream_count + stream_index
    moved = (position + shift) % ring
    tm_moved = (tm_index & ~2) | ((moved // stream_count) << 1)
    return tm_moved * stream_count + moved % stream_count


def ring_pull(value, shift):
    stream_count = lax.axis_size("stream")
    total = lax.axis_size("tm") * stream_count
    pairs = [(ring_source(target, shift, stream_count), target) for target in range(total)]
    return lax.ppermute(value, ("tm", "stream"), pairs)


def ring_gather(block):
    stream_count = lax.axis_size("stream")
    if stream_count != 4 or lax.axis_size("tm") % 4 or block.shape[1] % 256:
        return lax.all_gather(block, "stream", axis=0, tiled=True)
    rows, width = block.shape
    stream_index = lax.axis_index("stream")
    split = width // 2
    two_away = jnp.concatenate(
        [ring_pull(block[:, :split], 2), ring_pull(block[:, split:], -2)], axis=1
    )
    arrived = [block, ring_pull(block, 1), two_away, ring_pull(block, -1)]
    placed = []
    for position in range(stream_count):
        offset = (position - stream_index) % stream_count
        chosen = arrived[3]
        for slot in (2, 1, 0):
            chosen = jnp.where(offset == slot, arrived[slot], chosen)
        placed.append(chosen)
    return jnp.concatenate(placed, axis=0)


def contract_last(left, right):
    return lax.dot_general(
        left, right, (((1,), (1,)), ((), ())), preferred_element_type=jnp.float32
    )


def contract_first(left, right):
    return lax.dot_general(
        left, right, (((0,), (0,)), ((), ())), preferred_element_type=jnp.float32
    )


def per_device(series, loss_grad, query_weight, keyval_weight, output_weight, lengths):
    record_rows = series[0]
    outer_grad = loss_grad[0]
    valid_count = lengths[0]
    shard_tokens = record_rows.shape[0]
    keyval_width = keyval_weight.shape[1]
    key_width = keyval_width // 2
    group_size = HEADS // KV_HEADS
    tile_rows = min(128, shard_tokens)
    key_span = REACH * shard_tokens + tile_rows
    score_scale = HEAD_DIM ** (-0.5)
    anchor = lax.axis_index("tm") * shard_tokens
    query_width = query_weight.shape[1]
    weights_local = jnp.concatenate([query_weight, keyval_weight, output_weight], axis=1)
    if lax.axis_size("tm") % 2 == 0 and weights_local.shape[1] % 256 == 0:
        half_width = weights_local.shape[1] // 2
        core = lax.axis_index("tm") % 2
        mine = ring_gather(lax.dynamic_slice_in_dim(weights_local, core * half_width, half_width, 1))
        other = xor_swap(mine, "tm", 0)
        weights_full = jnp.concatenate(
            [jnp.where(core == 0, mine, other), jnp.where(core == 0, other, mine)], axis=1
        )
    else:
        weights_full = lax.all_gather(weights_local, "stream", axis=0, tiled=True)
    query_full = weights_full[:, :query_width]
    keyval_full = weights_full[:, query_width : query_width + keyval_width]
    output_full = weights_full[:, query_width + keyval_width :]
    queries = jnp.dot(record_rows, query_full, preferred_element_type=jnp.float32).astype(
        jnp.bfloat16
    )
    keyvals = jnp.dot(record_rows, keyval_full, preferred_element_type=jnp.float32).astype(
        jnp.bfloat16
    )
    attn_grad = contract_last(outer_grad, output_full).astype(jnp.bfloat16)
    earlier = [shifted(keyvals, "tm", offset) for offset in range(REACH, 0, -1)]
    window_keyvals = jnp.concatenate(earlier + [keyvals], axis=0)
    key_parts = []
    value_parts = []
    query_grads = []
    for head_group in range(KV_HEADS):
        query_cols = slice(
            head_group * group_size * HEAD_DIM, (head_group + 1) * group_size * HEAD_DIM
        )
        key_cols = slice(head_group * HEAD_DIM, (head_group + 1) * HEAD_DIM)
        value_cols = slice(
            key_width + head_group * HEAD_DIM, key_width + (head_group + 1) * HEAD_DIM
        )
        group_key = None
        group_value = None
        query_tile = queries[0:tile_rows, query_cols].reshape(tile_rows, group_size, HEAD_DIM)
        key_tile = window_keyvals[0:key_span, key_cols]
        value_tile = window_keyvals[0:key_span, value_cols]
        query_pos = anchor + 0 + jnp.arange(tile_rows, dtype=jnp.int32)
        key_pos = anchor - REACH * shard_tokens + 0 + jnp.arange(key_span, dtype=jnp.int32)
        live_rows = query_pos < valid_count
        allowed = (key_pos[None, :] <= query_pos[:, None]) & (
            query_pos[:, None] - key_pos[None, :] < REACH * shard_tokens
        )
        allowed = (
            allowed
            & (key_pos[None, :] >= 0)
            & (key_pos[None, :] < valid_count)
            & live_rows[:, None]
        )
        scores = (
            jnp.einsum("qjd,kd->jqk", query_tile, key_tile, preferred_element_type=jnp.float32)
            * score_scale
        )
        masked = jnp.where(allowed, scores, -1e30)
        row_max = jnp.max(masked, axis=-1, keepdims=True)
        terms = jnp.where(allowed, jnp.exp(masked - row_max), 0.0)
        denom = jnp.sum(terms, axis=-1, keepdims=True)
        denom = jnp.where(live_rows[:, None], denom, 1.0)
        attn_probs = (terms / denom).astype(jnp.bfloat16)
        attn_tile = jnp.einsum(
            "jqk,kd->qjd", attn_probs, value_tile, preferred_element_type=jnp.float32
        ).astype(jnp.bfloat16)
        grad_tile = attn_grad[0:tile_rows, query_cols].reshape(tile_rows, group_size, HEAD_DIM)
        row_delta = jnp.sum(
            grad_tile.astype(jnp.float32) * attn_tile.astype(jnp.float32), axis=-1
        ).T[:, :, None]
        prob_grad = jnp.einsum(
            "qjd,kd->jqk", grad_tile, value_tile, preferred_element_type=jnp.float32
        )
        score_grad = (
            attn_probs.astype(jnp.float32) * (prob_grad - row_delta) * score_scale
        ).astype(jnp.bfloat16)
        query_grad = jnp.einsum(
            "jqk,kd->qjd", score_grad, key_tile, preferred_element_type=jnp.float32
        ).astype(jnp.bfloat16)
        key_grad = jnp.einsum(
            "jqk,qjd->kd", score_grad, query_tile, preferred_element_type=jnp.float32
        )
        value_grad = jnp.einsum(
            "jqk,qjd->kd", attn_probs, grad_tile, preferred_element_type=jnp.float32
        )
        group_key = key_grad
        group_value = value_grad
        tile_list = query_grad.reshape(tile_rows, group_size * HEAD_DIM)
        key_parts.append(group_key)
        value_parts.append(group_value)
        query_grads.append(tile_list)
    query_grad_all = jnp.concatenate(query_grads, axis=1)
    partial_value = jnp.concatenate(key_parts + value_parts, axis=1)

    def shard_slot(offset):
        return partial_value[(REACH - offset) * shard_tokens : (REACH - offset + 1) * shard_tokens]

    summed = shard_slot(0)
    for offset in range(1, REACH + 1):
        summed = summed + shifted(shard_slot(offset).astype(jnp.bfloat16), "tm", -offset).astype(
            jnp.float32
        )
    keyval_grads = summed.astype(jnp.bfloat16)
    input_grad = contract_last(query_grad_all, query_full) + contract_last(
        keyval_grads, keyval_full
    )
    input_grad = input_grad.astype(jnp.bfloat16)
    weight_grad = grad_sum((record_rows, keyval_grads))
    return (input_grad[None], weight_grad)


def solution(mesh):
    placed = (
        P("stream", "tm", None),
        P("stream", "tm", None),
        P("stream", None),
        P("stream", None),
        P("stream", None),
        P("stream"),
    )
    return jax.shard_map(
        per_device,
        mesh=mesh,
        in_specs=placed,
        out_specs=(P("stream", "tm", None), P("stream", None)),
        check_vma=False,
    )
```

```python
import jax
import jax.numpy as jnp
from jax import lax
from jax.sharding import PartitionSpec as P

HEADS = 16
KV_HEADS = 4
HEAD_DIM = 64
REACH = 4


def shifted(value, axis, steps):
    count = lax.axis_size(axis)
    leading, last = (max(0, -steps), min(count, count - steps))
    return lax.ppermute(value, axis, [(source, source + steps) for source in range(leading, last)])


def xor_swap(value, axis, bit):
    count = lax.axis_size(axis)
    return lax.ppermute(value, axis, [(source, source ^ (1 << bit)) for source in range(count)])


def tree_psum(value, axis):
    count = lax.axis_size(axis)
    bits = count.bit_length() - 1
    if count != 1 << bits or value.shape[0] % count:
        return lax.psum(value, axis)
    order = [b for b in (0, 2, 4, 1, 3, 5, 6) if b < bits] + list(range(7, bits))
    index = lax.axis_index(axis)
    current = value
    for bit in order:
        half = current.shape[0] // 2
        upper = ((index >> bit) & 1) == 1
        low, high = current[:half], current[half:]
        keep = jnp.where(upper, high, low)
        send = jnp.where(upper, low, high)
        current = keep + xor_swap(send, axis, bit)
    for bit in reversed(order):
        upper = ((index >> bit) & 1) == 1
        other = xor_swap(current, axis, bit)
        current = jnp.where(
            upper, jnp.concatenate([other, current]), jnp.concatenate([current, other])
        )
    return current


def halve_stage(value, axis, bit, wire):
    half = value.shape[0] // 2
    upper = ((lax.axis_index(axis) >> bit) & 1) == 1
    low, high = value[:half], value[half:]
    keep = jnp.where(upper, high, low).astype(jnp.float32)
    send = jnp.where(upper, low, high)
    return keep + xor_swap(send.astype(wire), axis, bit).astype(jnp.float32)


def double_stage(value, axis, bit):
    upper = ((lax.axis_index(axis) >> bit) & 1) == 1
    other = xor_swap(value, axis, bit)
    return jnp.where(upper, jnp.concatenate([other, value]), jnp.concatenate([value, other]))


NEAR_BITS = (2, 4)


def grad_sum(partial):
    stream_count = lax.axis_size("stream")
    tm_count = lax.axis_size("tm")
    stream_bits = stream_count.bit_length() - 1
    tm_bits = tm_count.bit_length() - 1
    rows, grads = partial
    tokens, features = rows.shape
    if (
        stream_count != 1 << stream_bits
        or tm_count != 1 << tm_bits
        or stream_bits == 0
        or tm_bits == 0
        or features % (2 * stream_count)
        or grads.shape[1] % 256
    ):
        shard = lax.psum_scatter(
            contract_first(rows, grads).astype(jnp.bfloat16), "stream", scatter_dimension=0, tiled=True
        ).astype(jnp.float32)
        return lax.psum(shard, "tm")
    stream_index = lax.axis_index("stream")
    core = lax.axis_index("tm") % 2
    half_cols = grads.shape[1] // 2
    paired = rows.reshape(tokens, stream_count // 2, 2, features // stream_count)
    even = paired[:, :, 0].reshape(tokens, features // 2)
    odd = paired[:, :, 1].reshape(tokens, features // 2)
    upper = (stream_index & 1) == 1
    ordered = jnp.concatenate([jnp.where(upper, odd, even), jnp.where(upper, even, odd)], axis=1)
    mine_cols = lax.dynamic_slice_in_dim(grads, core * half_cols, half_cols, 1)
    other_cols = lax.dynamic_slice_in_dim(grads, (1 - core) * half_cols, half_cols, 1)
    current = contract_first(ordered, mine_cols) + xor_swap(
        contract_first(ordered, other_cols).astype(jnp.bfloat16), "tm", 0
    ).astype(jnp.float32)
    half_rows = features // 2
    current = current[:half_rows] + xor_swap(
        current[half_rows:].astype(jnp.bfloat16), "stream", 0
    ).astype(jnp.float32)
    for bit in reversed(range(1, stream_bits)):
        current = halve_stage(current, "stream", bit, jnp.bfloat16)
    near = [bit for bit in NEAR_BITS if bit < tm_bits]
    near = near[: max(0, current.shape[0].bit_length() - 1)]
    for bit in near:
        current = halve_stage(current, "tm", bit, jnp.float32)
    for bit in range(1, tm_bits):
        if bit not in near:
            current = current + xor_swap(current, "tm", bit)
    for bit in reversed(near):
        current = double_stage(current, "tm", bit)
    other = xor_swap(current, "tm", 0)
    return jnp.where(
        core == 1,
        jnp.concatenate([other, current], axis=1),
        jnp.concatenate([current, other], axis=1),
    )


def ring_source(linear, shift, stream_count):
    tm_index, stream_index = divmod(linear, stream_count)
    ring = 2 * stream_count
    position = ((tm_index >> 1) & 1) * stream_count + stream_index
    moved = (position + shift) % ring
    tm_moved = (tm_index & ~2) | ((moved // stream_count) << 1)
    return tm_moved * stream_count + moved % stream_count


def ring_pull(value, shift):
    stream_count = lax.axis_size("stream")
    total = lax.axis_size("tm") * stream_count
    pairs = [(ring_source(target, shift, stream_count), target) for target in range(total)]
    return lax.ppermute(value, ("tm", "stream"), pairs)


def ring_gather(block):
    stream_count = lax.axis_size("stream")
    if stream_count != 4 or lax.axis_size("tm") % 4 or block.shape[1] % 256:
        return lax.all_gather(block, "stream", axis=0, tiled=True)
    rows, width = block.shape
    stream_index = lax.axis_index("stream")
    split = width // 2
    two_away = jnp.concatenate(
        [ring_pull(block[:, :split], 2), ring_pull(block[:, split:], -2)], axis=1
    )
    arrived = [block, ring_pull(block, 1), two_away, ring_pull(block, -1)]
    placed = []
    for position in range(stream_count):
        offset = (position - stream_index) % stream_count
        chosen = arrived[3]
        for slot in (2, 1, 0):
            chosen = jnp.where(offset == slot, arrived[slot], chosen)
        placed.append(chosen)
    return jnp.concatenate(placed, axis=0)


def contract_last(left, right):
    return lax.dot_general(
        left, right, (((1,), (1,)), ((), ())), preferred_element_type=jnp.float32
    )


def contract_first(left, right):
    return lax.dot_general(
        left, right, (((0,), (0,)), ((), ())), preferred_element_type=jnp.float32
    )


def per_device(series, loss_grad, query_weight, keyval_weight, output_weight, lengths):
    record_rows = series[0]
    outer_grad = loss_grad[0]
    valid_count = lengths[0]
    shard_tokens = record_rows.shape[0]
    keyval_width = keyval_weight.shape[1]
    key_width = keyval_width // 2
    group_size = HEADS // KV_HEADS
    tile_rows = min(128, shard_tokens)
    key_span = REACH * shard_tokens + tile_rows
    score_scale = HEAD_DIM ** (-0.5)
    anchor = lax.axis_index("tm") * shard_tokens
    query_width = query_weight.shape[1]
    weights_local = jnp.concatenate([query_weight, keyval_weight, output_weight], axis=1)
    if lax.axis_size("tm") % 2 == 0 and weights_local.shape[1] % 256 == 0:
        half_width = weights_local.shape[1] // 2
        core = lax.axis_index("tm") % 2
        mine = ring_gather(lax.dynamic_slice_in_dim(weights_local, core * half_width, half_width, 1))
        other = xor_swap(mine, "tm", 0)
        weights_full = jnp.concatenate(
            [jnp.where(core == 0, mine, other), jnp.where(core == 0, other, mine)], axis=1
        )
    else:
        weights_full = lax.all_gather(weights_local, "stream", axis=0, tiled=True)
    query_full = weights_full[:, :query_width]
    keyval_full = weights_full[:, query_width : query_width + keyval_width]
    output_full = weights_full[:, query_width + keyval_width :]
    queries = jnp.dot(record_rows, query_full, preferred_element_type=jnp.float32).astype(
        jnp.bfloat16
    )
    keyvals = jnp.dot(record_rows, keyval_full, preferred_element_type=jnp.float32).astype(
        jnp.bfloat16
    )
    attn_grad = contract_last(outer_grad, output_full).astype(jnp.bfloat16)
    earlier = [shifted(keyvals, "tm", offset) for offset in range(REACH, 0, -1)]
    window_keyvals = jnp.concatenate(earlier + [keyvals], axis=0)
    query_block = queries[0:tile_rows].reshape(tile_rows, KV_HEADS, group_size, HEAD_DIM)
    key_block = window_keyvals[0:key_span, :key_width].reshape(key_span, KV_HEADS, HEAD_DIM)
    value_block = window_keyvals[0:key_span, key_width:].reshape(key_span, KV_HEADS, HEAD_DIM)
    query_pos = anchor + jnp.arange(tile_rows, dtype=jnp.int32)
    key_pos = anchor - REACH * shard_tokens + jnp.arange(key_span, dtype=jnp.int32)
    live_rows = query_pos < valid_count
    allowed = (key_pos[None, :] <= query_pos[:, None]) & (
        query_pos[:, None] - key_pos[None, :] < REACH * shard_tokens
    )
    allowed = (
        allowed
        & (key_pos[None, :] >= 0)
        & (key_pos[None, :] < valid_count)
        & live_rows[:, None]
    )
    scores = (
        jnp.einsum("qgjd,kgd->gjqk", query_block, key_block, preferred_element_type=jnp.float32)
        * score_scale
    )
    masked = jnp.where(allowed, scores, -1e30)
    row_max = jnp.max(masked, axis=-1, keepdims=True)
    terms = jnp.where(allowed, jnp.exp(masked - row_max), 0.0)
    denom = jnp.sum(terms, axis=-1, keepdims=True)
    denom = jnp.where(live_rows[:, None], denom, 1.0)
    attn_probs = (terms / denom).astype(jnp.bfloat16)
    attn_block = jnp.einsum(
        "gjqk,kgd->qgjd", attn_probs, value_block, preferred_element_type=jnp.float32
    ).astype(jnp.bfloat16)
    grad_block = attn_grad[0:tile_rows].reshape(tile_rows, KV_HEADS, group_size, HEAD_DIM)
    row_delta = jnp.transpose(
        jnp.sum(grad_block.astype(jnp.float32) * attn_block.astype(jnp.float32), axis=-1),
        (1, 2, 0),
    )[..., None]
    prob_grad = jnp.einsum(
        "qgjd,kgd->gjqk", grad_block, value_block, preferred_element_type=jnp.float32
    )
    score_grad = (
        attn_probs.astype(jnp.float32) * (prob_grad - row_delta) * score_scale
    ).astype(jnp.bfloat16)
    query_grad_all = (
        jnp.einsum("gjqk,kgd->qgjd", score_grad, key_block, preferred_element_type=jnp.float32)
        .astype(jnp.bfloat16)
        .reshape(tile_rows, KV_HEADS * group_size * HEAD_DIM)
    )
    key_grad = jnp.einsum(
        "gjqk,qgjd->kgd", score_grad, query_block, preferred_element_type=jnp.float32
    ).reshape(key_span, key_width)
    value_grad = jnp.einsum(
        "gjqk,qgjd->kgd", attn_probs, grad_block, preferred_element_type=jnp.float32
    ).reshape(key_span, key_width)
    partial_value = jnp.concatenate([key_grad, value_grad], axis=1)

    def shard_slot(offset):
        return partial_value[(REACH - offset) * shard_tokens : (REACH - offset + 1) * shard_tokens]

    summed = shard_slot(0)
    for offset in range(1, REACH + 1):
        summed = summed + shifted(shard_slot(offset).astype(jnp.bfloat16), "tm", -offset).astype(
            jnp.float32
        )
    keyval_grads = summed.astype(jnp.bfloat16)
    input_grad = contract_last(query_grad_all, query_full) + contract_last(
        keyval_grads, keyval_full
    )
    input_grad = input_grad.astype(jnp.bfloat16)
    weight_grad = grad_sum((record_rows, keyval_grads))
    return (input_grad[None], weight_grad)


def solution(mesh):
    placed = (
        P("stream", "tm", None),
        P("stream", "tm", None),
        P("stream", None),
        P("stream", None),
        P("stream", None),
        P("stream"),
    )
    return jax.shard_map(
        per_device,
        mesh=mesh,
        in_specs=placed,
        out_specs=(P("stream", "tm", None), P("stream", None)),
        check_vma=False,
    )
```

```python
import jax
import jax.numpy as jnp
from jax import lax
from jax.sharding import PartitionSpec as P

HEADS = 16
KV_HEADS = 4
HEAD_DIM = 64
REACH = 4


def shifted(value, axis, steps):
    count = lax.axis_size(axis)
    leading, last = (max(0, -steps), min(count, count - steps))
    return lax.ppermute(value, axis, [(source, source + steps) for source in range(leading, last)])


def xor_swap(value, axis, bit):
    count = lax.axis_size(axis)
    return lax.ppermute(value, axis, [(source, source ^ (1 << bit)) for source in range(count)])


def tree_psum(value, axis):
    count = lax.axis_size(axis)
    bits = count.bit_length() - 1
    if count != 1 << bits or value.shape[0] % count:
        return lax.psum(value, axis)
    order = [b for b in (0, 2, 4, 1, 3, 5, 6) if b < bits] + list(range(7, bits))
    index = lax.axis_index(axis)
    current = value
    for bit in order:
        half = current.shape[0] // 2
        upper = ((index >> bit) & 1) == 1
        low, high = current[:half], current[half:]
        keep = jnp.where(upper, high, low)
        send = jnp.where(upper, low, high)
        current = keep + xor_swap(send, axis, bit)
    for bit in reversed(order):
        upper = ((index >> bit) & 1) == 1
        other = xor_swap(current, axis, bit)
        current = jnp.where(
            upper, jnp.concatenate([other, current]), jnp.concatenate([current, other])
        )
    return current


def halve_stage(value, axis, bit, wire):
    half = value.shape[0] // 2
    upper = ((lax.axis_index(axis) >> bit) & 1) == 1
    low, high = value[:half], value[half:]
    keep = jnp.where(upper, high, low).astype(jnp.float32)
    send = jnp.where(upper, low, high)
    return keep + xor_swap(send.astype(wire), axis, bit).astype(jnp.float32)


def double_stage(value, axis, bit):
    upper = ((lax.axis_index(axis) >> bit) & 1) == 1
    other = xor_swap(value, axis, bit)
    return jnp.where(upper, jnp.concatenate([other, value]), jnp.concatenate([value, other]))


NEAR_BITS = (2, 4)


def grad_sum(partial):
    stream_count = lax.axis_size("stream")
    tm_count = lax.axis_size("tm")
    stream_bits = stream_count.bit_length() - 1
    tm_bits = tm_count.bit_length() - 1
    rows, grads = partial
    tokens, features = rows.shape
    if (
        stream_count != 1 << stream_bits
        or tm_count != 1 << tm_bits
        or stream_bits == 0
        or tm_bits == 0
        or features % (2 * stream_count)
        or grads.shape[1] % 256
    ):
        shard = lax.psum_scatter(
            contract_first(rows, grads).astype(jnp.bfloat16), "stream", scatter_dimension=0, tiled=True
        ).astype(jnp.float32)
        return lax.psum(shard, "tm")
    stream_index = lax.axis_index("stream")
    core = lax.axis_index("tm") % 2
    half_cols = grads.shape[1] // 2
    paired = rows.reshape(tokens, stream_count // 2, 2, features // stream_count)
    even = paired[:, :, 0].reshape(tokens, features // 2)
    odd = paired[:, :, 1].reshape(tokens, features // 2)
    upper = (stream_index & 1) == 1
    ordered = jnp.concatenate([jnp.where(upper, odd, even), jnp.where(upper, even, odd)], axis=1)
    mine_cols = lax.dynamic_slice_in_dim(grads, core * half_cols, half_cols, 1)
    other_cols = lax.dynamic_slice_in_dim(grads, (1 - core) * half_cols, half_cols, 1)
    current = contract_first(ordered, mine_cols) + xor_swap(
        contract_first(ordered, other_cols).astype(jnp.bfloat16), "tm", 0
    ).astype(jnp.float32)
    half_rows = features // 2
    current = current[:half_rows] + xor_swap(
        current[half_rows:].astype(jnp.bfloat16), "stream", 0
    ).astype(jnp.float32)
    for bit in reversed(range(1, stream_bits)):
        current = halve_stage(current, "stream", bit, jnp.bfloat16)
    near = [bit for bit in NEAR_BITS if bit < tm_bits]
    near = near[: max(0, current.shape[0].bit_length() - 1)]
    for bit in near:
        current = halve_stage(current, "tm", bit, jnp.bfloat16)
    for bit in range(1, tm_bits):
        if bit not in near:
            rounded = current.astype(jnp.bfloat16)
            current = rounded.astype(jnp.float32) + xor_swap(rounded, "tm", bit).astype(jnp.float32)
    for bit in reversed(near):
        current = double_stage(current, "tm", bit)
    other = xor_swap(current, "tm", 0)
    return jnp.where(
        core == 1,
        jnp.concatenate([other, current], axis=1),
        jnp.concatenate([current, other], axis=1),
    )


def ring_source(linear, shift, stream_count):
    tm_index, stream_index = divmod(linear, stream_count)
    ring = 2 * stream_count
    position = ((tm_index >> 1) & 1) * stream_count + stream_index
    moved = (position + shift) % ring
    tm_moved = (tm_index & ~2) | ((moved // stream_count) << 1)
    return tm_moved * stream_count + moved % stream_count


def ring_pull(value, shift):
    stream_count = lax.axis_size("stream")
    total = lax.axis_size("tm") * stream_count
    pairs = [(ring_source(target, shift, stream_count), target) for target in range(total)]
    return lax.ppermute(value, ("tm", "stream"), pairs)


def ring_gather(block):
    stream_count = lax.axis_size("stream")
    if stream_count != 4 or lax.axis_size("tm") % 4 or block.shape[1] % 256:
        return lax.all_gather(block, "stream", axis=0, tiled=True)
    rows, width = block.shape
    stream_index = lax.axis_index("stream")
    split = width // 2
    two_away = jnp.concatenate(
        [ring_pull(block[:, :split], 2), ring_pull(block[:, split:], -2)], axis=1
    )
    arrived = [block, ring_pull(block, 1), two_away, ring_pull(block, -1)]
    placed = []
    for position in range(stream_count):
        offset = (position - stream_index) % stream_count
        chosen = arrived[3]
        for slot in (2, 1, 0):
            chosen = jnp.where(offset == slot, arrived[slot], chosen)
        placed.append(chosen)
    return jnp.concatenate(placed, axis=0)


def contract_last(left, right):
    return lax.dot_general(
        left, right, (((1,), (1,)), ((), ())), preferred_element_type=jnp.float32
    )


def contract_first(left, right):
    return lax.dot_general(
        left, right, (((0,), (0,)), ((), ())), preferred_element_type=jnp.float32
    )


def per_device(series, loss_grad, query_weight, keyval_weight, output_weight, lengths):
    record_rows = series[0]
    outer_grad = loss_grad[0]
    valid_count = lengths[0]
    shard_tokens = record_rows.shape[0]
    keyval_width = keyval_weight.shape[1]
    key_width = keyval_width // 2
    group_size = HEADS // KV_HEADS
    tile_rows = min(128, shard_tokens)
    key_span = REACH * shard_tokens + tile_rows
    score_scale = HEAD_DIM ** (-0.5)
    anchor = lax.axis_index("tm") * shard_tokens
    query_width = query_weight.shape[1]
    weights_local = jnp.concatenate([query_weight, keyval_weight, output_weight], axis=1)
    if lax.axis_size("tm") % 2 == 0 and weights_local.shape[1] % 256 == 0:
        half_width = weights_local.shape[1] // 2
        core = lax.axis_index("tm") % 2
        mine = ring_gather(lax.dynamic_slice_in_dim(weights_local, core * half_width, half_width, 1))
        other = xor_swap(mine, "tm", 0)
        weights_full = jnp.concatenate(
            [jnp.where(core == 0, mine, other), jnp.where(core == 0, other, mine)], axis=1
        )
    else:
        weights_full = lax.all_gather(weights_local, "stream", axis=0, tiled=True)
    query_full = weights_full[:, :query_width]
    keyval_full = weights_full[:, query_width : query_width + keyval_width]
    output_full = weights_full[:, query_width + keyval_width :]
    queries = jnp.dot(record_rows, query_full, preferred_element_type=jnp.float32).astype(
        jnp.bfloat16
    )
    keyvals = jnp.dot(record_rows, keyval_full, preferred_element_type=jnp.float32).astype(
        jnp.bfloat16
    )
    attn_grad = contract_last(outer_grad, output_full).astype(jnp.bfloat16)
    earlier = [shifted(keyvals, "tm", offset) for offset in range(REACH, 0, -1)]
    window_keyvals = jnp.concatenate(earlier + [keyvals], axis=0)
    query_block = queries[0:tile_rows].reshape(tile_rows, KV_HEADS, group_size, HEAD_DIM)
    key_block = window_keyvals[0:key_span, :key_width].reshape(key_span, KV_HEADS, HEAD_DIM)
    value_block = window_keyvals[0:key_span, key_width:].reshape(key_span, KV_HEADS, HEAD_DIM)
    query_pos = anchor + jnp.arange(tile_rows, dtype=jnp.int32)
    key_pos = anchor - REACH * shard_tokens + jnp.arange(key_span, dtype=jnp.int32)
    live_rows = query_pos < valid_count
    allowed = (key_pos[None, :] <= query_pos[:, None]) & (
        query_pos[:, None] - key_pos[None, :] < REACH * shard_tokens
    )
    allowed = (
        allowed
        & (key_pos[None, :] >= 0)
        & (key_pos[None, :] < valid_count)
        & live_rows[:, None]
    )
    scores = (
        jnp.einsum("qgjd,kgd->gjqk", query_block, key_block, preferred_element_type=jnp.float32)
        * score_scale
    )
    masked = jnp.where(allowed, scores, -1e30)
    row_max = jnp.max(masked, axis=-1, keepdims=True)
    terms = jnp.where(allowed, jnp.exp(masked - row_max), 0.0)
    denom = jnp.sum(terms, axis=-1, keepdims=True)
    denom = jnp.where(live_rows[:, None], denom, 1.0)
    attn_probs = (terms / denom).astype(jnp.bfloat16)
    attn_block = jnp.einsum(
        "gjqk,kgd->qgjd", attn_probs, value_block, preferred_element_type=jnp.float32
    ).astype(jnp.bfloat16)
    grad_block = attn_grad[0:tile_rows].reshape(tile_rows, KV_HEADS, group_size, HEAD_DIM)
    row_delta = jnp.transpose(
        jnp.sum(grad_block.astype(jnp.float32) * attn_block.astype(jnp.float32), axis=-1),
        (1, 2, 0),
    )[..., None]
    prob_grad = jnp.einsum(
        "qgjd,kgd->gjqk", grad_block, value_block, preferred_element_type=jnp.float32
    )
    score_grad = (
        attn_probs.astype(jnp.float32) * (prob_grad - row_delta) * score_scale
    ).astype(jnp.bfloat16)
    query_grad_all = (
        jnp.einsum("gjqk,kgd->qgjd", score_grad, key_block, preferred_element_type=jnp.float32)
        .astype(jnp.bfloat16)
        .reshape(tile_rows, KV_HEADS * group_size * HEAD_DIM)
    )
    key_grad = jnp.einsum(
        "gjqk,qgjd->kgd", score_grad, query_block, preferred_element_type=jnp.float32
    ).reshape(key_span, key_width)
    value_grad = jnp.einsum(
        "gjqk,qgjd->kgd", attn_probs, grad_block, preferred_element_type=jnp.float32
    ).reshape(key_span, key_width)
    partial_value = jnp.concatenate([key_grad, value_grad], axis=1)

    def shard_slot(offset):
        return partial_value[(REACH - offset) * shard_tokens : (REACH - offset + 1) * shard_tokens]

    summed = shard_slot(0)
    for offset in range(1, REACH + 1):
        summed = summed + shifted(shard_slot(offset).astype(jnp.bfloat16), "tm", -offset).astype(
            jnp.float32
        )
    keyval_grads = summed.astype(jnp.bfloat16)
    input_grad = contract_last(query_grad_all, query_full) + contract_last(
        keyval_grads, keyval_full
    )
    input_grad = input_grad.astype(jnp.bfloat16)
    weight_grad = grad_sum((record_rows, keyval_grads))
    return (input_grad[None], weight_grad)


def solution(mesh):
    placed = (
        P("stream", "tm", None),
        P("stream", "tm", None),
        P("stream", None),
        P("stream", None),
        P("stream", None),
        P("stream"),
    )
    return jax.shard_map(
        per_device,
        mesh=mesh,
        in_specs=placed,
        out_specs=(P("stream", "tm", None), P("stream", None)),
        check_vma=False,
    )
```

```python
import jax
import jax.numpy as jnp
from jax import lax
from jax.sharding import PartitionSpec as P

HEADS = 16
KV_HEADS = 4
HEAD_DIM = 64
REACH = 4


def shifted(value, axis, steps):
    count = lax.axis_size(axis)
    leading, last = (max(0, -steps), min(count, count - steps))
    return lax.ppermute(value, axis, [(source, source + steps) for source in range(leading, last)])


def xor_swap(value, axis, bit):
    count = lax.axis_size(axis)
    return lax.ppermute(value, axis, [(source, source ^ (1 << bit)) for source in range(count)])


def tree_psum(value, axis):
    count = lax.axis_size(axis)
    bits = count.bit_length() - 1
    if count != 1 << bits or value.shape[0] % count:
        return lax.psum(value, axis)
    order = [b for b in (0, 2, 4, 1, 3, 5, 6) if b < bits] + list(range(7, bits))
    index = lax.axis_index(axis)
    current = value
    for bit in order:
        half = current.shape[0] // 2
        upper = ((index >> bit) & 1) == 1
        low, high = current[:half], current[half:]
        keep = jnp.where(upper, high, low)
        send = jnp.where(upper, low, high)
        current = keep + xor_swap(send, axis, bit)
    for bit in reversed(order):
        upper = ((index >> bit) & 1) == 1
        other = xor_swap(current, axis, bit)
        current = jnp.where(
            upper, jnp.concatenate([other, current]), jnp.concatenate([current, other])
        )
    return current


def halve_stage(value, axis, bit, wire):
    half = value.shape[0] // 2
    upper = ((lax.axis_index(axis) >> bit) & 1) == 1
    low, high = value[:half], value[half:]
    keep = jnp.where(upper, high, low).astype(jnp.float32)
    send = jnp.where(upper, low, high)
    return keep + xor_swap(send.astype(wire), axis, bit).astype(jnp.float32)


def double_stage(value, axis, bit):
    upper = ((lax.axis_index(axis) >> bit) & 1) == 1
    other = xor_swap(value, axis, bit)
    return jnp.where(upper, jnp.concatenate([other, value]), jnp.concatenate([value, other]))


NEAR_BITS = (2, 4)


def grad_sum(partial):
    stream_count = lax.axis_size("stream")
    tm_count = lax.axis_size("tm")
    stream_bits = stream_count.bit_length() - 1
    tm_bits = tm_count.bit_length() - 1
    rows, grads = partial
    tokens, features = rows.shape
    if (
        stream_count != 1 << stream_bits
        or tm_count != 1 << tm_bits
        or stream_bits == 0
        or tm_bits == 0
        or features % (2 * stream_count)
        or grads.shape[1] % 256
    ):
        shard = lax.psum_scatter(
            contract_first(rows, grads).astype(jnp.bfloat16), "stream", scatter_dimension=0, tiled=True
        ).astype(jnp.float32)
        return lax.psum(shard, "tm")
    stream_index = lax.axis_index("stream")
    core = lax.axis_index("tm") % 2
    half_cols = grads.shape[1] // 2
    paired = rows.reshape(tokens, stream_count // 2, 2, features // stream_count)
    even = paired[:, :, 0].reshape(tokens, features // 2)
    odd = paired[:, :, 1].reshape(tokens, features // 2)
    upper = (stream_index & 1) == 1
    ordered = jnp.concatenate([jnp.where(upper, odd, even), jnp.where(upper, even, odd)], axis=1)
    mine_cols = lax.dynamic_slice_in_dim(grads, core * half_cols, half_cols, 1)
    other_cols = lax.dynamic_slice_in_dim(grads, (1 - core) * half_cols, half_cols, 1)
    current = contract_first(ordered, mine_cols) + xor_swap(
        contract_first(ordered, other_cols).astype(jnp.bfloat16), "tm", 0
    ).astype(jnp.float32)
    half_rows = features // 2
    current = current[:half_rows] + xor_swap(
        current[half_rows:].astype(jnp.bfloat16), "stream", 0
    ).astype(jnp.float32)
    for bit in reversed(range(1, stream_bits)):
        current = halve_stage(current, "stream", bit, jnp.bfloat16)
    near = [bit for bit in NEAR_BITS if bit < tm_bits]
    near = near[: max(0, current.shape[0].bit_length() - 1)]
    for bit in near:
        current = halve_stage(current, "tm", bit, jnp.bfloat16)
    for bit in range(1, tm_bits):
        if bit not in near:
            rounded = current.astype(jnp.bfloat16)
            current = rounded.astype(jnp.float32) + xor_swap(rounded, "tm", bit).astype(jnp.float32)
    for bit in reversed(near):
        current = double_stage(current, "tm", bit)
    other = xor_swap(current, "tm", 0)
    return jnp.where(
        core == 1,
        jnp.concatenate([other, current], axis=1),
        jnp.concatenate([current, other], axis=1),
    )


def ring_source(linear, shift, stream_count):
    tm_index, stream_index = divmod(linear, stream_count)
    ring = 2 * stream_count
    position = ((tm_index >> 1) & 1) * stream_count + stream_index
    moved = (position + shift) % ring
    tm_moved = (tm_index & ~2) | ((moved // stream_count) << 1)
    return tm_moved * stream_count + moved % stream_count


def ring_pull(value, shift):
    stream_count = lax.axis_size("stream")
    total = lax.axis_size("tm") * stream_count
    pairs = [(ring_source(target, shift, stream_count), target) for target in range(total)]
    return lax.ppermute(value, ("tm", "stream"), pairs)


def ring_gather(block):
    stream_count = lax.axis_size("stream")
    if stream_count != 4 or lax.axis_size("tm") % 4 or block.shape[1] % 256:
        return lax.all_gather(block, "stream", axis=0, tiled=True)
    rows, width = block.shape
    stream_index = lax.axis_index("stream")
    split = width // 2
    two_away = jnp.concatenate(
        [ring_pull(block[:, :split], 2), ring_pull(block[:, split:], -2)], axis=1
    )
    arrived = [block, ring_pull(block, 1), two_away, ring_pull(block, -1)]
    placed = []
    for position in range(stream_count):
        offset = (position - stream_index) % stream_count
        chosen = arrived[3]
        for slot in (2, 1, 0):
            chosen = jnp.where(offset == slot, arrived[slot], chosen)
        placed.append(chosen)
    return jnp.concatenate(placed, axis=0)


def contract_last(left, right):
    return lax.dot_general(
        left, right, (((1,), (1,)), ((), ())), preferred_element_type=jnp.float32
    )


def contract_first(left, right):
    return lax.dot_general(
        left, right, (((0,), (0,)), ((), ())), preferred_element_type=jnp.float32
    )


def per_device(series, loss_grad, query_weight, keyval_weight, output_weight, lengths):
    record_rows = series[0]
    outer_grad = loss_grad[0]
    valid_count = lengths[0]
    shard_tokens = record_rows.shape[0]
    keyval_width = keyval_weight.shape[1]
    key_width = keyval_width // 2
    group_size = HEADS // KV_HEADS
    tile_rows = min(128, shard_tokens)
    key_span = REACH * shard_tokens + tile_rows
    score_scale = HEAD_DIM ** (-0.5)
    anchor = lax.axis_index("tm") * shard_tokens
    query_width = query_weight.shape[1]
    weights_local = jnp.concatenate([query_weight, keyval_weight, output_weight], axis=1)
    if lax.axis_size("tm") % 2 == 0 and weights_local.shape[1] % 256 == 0:
        half_width = weights_local.shape[1] // 2
        core = lax.axis_index("tm") % 2
        mine = ring_gather(lax.dynamic_slice_in_dim(weights_local, core * half_width, half_width, 1))
        other = xor_swap(mine, "tm", 0)
        weights_full = jnp.concatenate(
            [jnp.where(core == 0, mine, other), jnp.where(core == 0, other, mine)], axis=1
        )
    else:
        weights_full = lax.all_gather(weights_local, "stream", axis=0, tiled=True)
    query_full = weights_full[:, :query_width]
    keyval_full = weights_full[:, query_width : query_width + keyval_width]
    output_full = weights_full[:, query_width + keyval_width :]
    queries = jnp.dot(record_rows, query_full, preferred_element_type=jnp.float32).astype(
        jnp.bfloat16
    )
    keyvals = jnp.dot(record_rows, keyval_full, preferred_element_type=jnp.float32).astype(
        jnp.bfloat16
    )
    attn_grad = contract_last(outer_grad, output_full).astype(jnp.bfloat16)
    earlier = [shifted(keyvals, "tm", offset) for offset in range(REACH, 0, -1)]
    window_keyvals = jnp.concatenate(earlier + [keyvals], axis=0)
    query_block = queries[0:tile_rows].reshape(tile_rows, KV_HEADS, group_size, HEAD_DIM)
    key_block = window_keyvals[0:key_span, :key_width].reshape(key_span, KV_HEADS, HEAD_DIM)
    value_block = window_keyvals[0:key_span, key_width:].reshape(key_span, KV_HEADS, HEAD_DIM)
    query_pos = anchor + jnp.arange(tile_rows, dtype=jnp.int32)
    key_pos = anchor - REACH * shard_tokens + jnp.arange(key_span, dtype=jnp.int32)
    live_rows = query_pos < valid_count
    allowed = (key_pos[None, :] <= query_pos[:, None]) & (
        query_pos[:, None] - key_pos[None, :] < REACH * shard_tokens
    )
    allowed = (
        allowed
        & (key_pos[None, :] >= 0)
        & (key_pos[None, :] < valid_count)
        & live_rows[:, None]
    )
    scores = (
        jnp.einsum("qgjd,kgd->gjqk", query_block, key_block, preferred_element_type=jnp.float32)
        * score_scale
    )
    masked = jnp.where(allowed, scores, -1e30)
    row_max = jnp.max(masked, axis=-1, keepdims=True)
    terms = jnp.where(allowed, jnp.exp(masked - row_max), 0.0)
    denom = jnp.sum(terms, axis=-1, keepdims=True)
    denom = jnp.where(live_rows[:, None], denom, 1.0)
    attn_probs = (terms * (1.0 / denom)).astype(jnp.bfloat16)
    attn_block = jnp.einsum(
        "gjqk,kgd->qgjd", attn_probs, value_block, preferred_element_type=jnp.float32
    ).astype(jnp.bfloat16)
    grad_block = attn_grad[0:tile_rows].reshape(tile_rows, KV_HEADS, group_size, HEAD_DIM)
    row_delta = jnp.transpose(
        jnp.sum(grad_block.astype(jnp.float32) * attn_block.astype(jnp.float32), axis=-1),
        (1, 2, 0),
    )[..., None]
    prob_grad = jnp.einsum(
        "qgjd,kgd->gjqk", grad_block, value_block, preferred_element_type=jnp.float32
    )
    score_grad = (
        attn_probs.astype(jnp.float32) * (prob_grad - row_delta) * score_scale
    ).astype(jnp.bfloat16)
    query_grad_all = (
        jnp.einsum("gjqk,kgd->qgjd", score_grad, key_block, preferred_element_type=jnp.float32)
        .astype(jnp.bfloat16)
        .reshape(tile_rows, KV_HEADS * group_size * HEAD_DIM)
    )
    key_grad = jnp.einsum(
        "gjqk,qgjd->kgd", score_grad, query_block, preferred_element_type=jnp.float32
    ).reshape(key_span, key_width)
    value_grad = jnp.einsum(
        "gjqk,qgjd->kgd", attn_probs, grad_block, preferred_element_type=jnp.float32
    ).reshape(key_span, key_width)
    partial_value = jnp.concatenate([key_grad, value_grad], axis=1)

    def shard_slot(offset):
        return partial_value[(REACH - offset) * shard_tokens : (REACH - offset + 1) * shard_tokens]

    summed = shard_slot(0)
    for offset in range(1, REACH + 1):
        summed = summed + shifted(shard_slot(offset).astype(jnp.bfloat16), "tm", -offset).astype(
            jnp.float32
        )
    keyval_grads = summed.astype(jnp.bfloat16)
    input_grad = contract_last(query_grad_all, query_full) + contract_last(
        keyval_grads, keyval_full
    )
    input_grad = input_grad.astype(jnp.bfloat16)
    weight_grad = grad_sum((record_rows, keyval_grads))
    return (input_grad[None], weight_grad)


def solution(mesh):
    placed = (
        P("stream", "tm", None),
        P("stream", "tm", None),
        P("stream", None),
        P("stream", None),
        P("stream", None),
        P("stream"),
    )
    return jax.shard_map(
        per_device,
        mesh=mesh,
        in_specs=placed,
        out_specs=(P("stream", "tm", None), P("stream", None)),
        check_vma=False,
    )
```

```python
import jax
import jax.numpy as jnp
from jax import lax
from jax.sharding import PartitionSpec as P

HEADS = 16
KV_HEADS = 4
HEAD_DIM = 64
REACH = 4


def shifted(value, axis, steps):
    count = lax.axis_size(axis)
    leading, last = (max(0, -steps), min(count, count - steps))
    return lax.ppermute(value, axis, [(source, source + steps) for source in range(leading, last)])


def xor_swap(value, axis, bit):
    count = lax.axis_size(axis)
    return lax.ppermute(value, axis, [(source, source ^ (1 << bit)) for source in range(count)])


def tree_psum(value, axis):
    count = lax.axis_size(axis)
    bits = count.bit_length() - 1
    if count != 1 << bits or value.shape[0] % count:
        return lax.psum(value, axis)
    order = [b for b in (0, 2, 4, 1, 3, 5, 6) if b < bits] + list(range(7, bits))
    index = lax.axis_index(axis)
    current = value
    for bit in order:
        half = current.shape[0] // 2
        upper = ((index >> bit) & 1) == 1
        low, high = current[:half], current[half:]
        keep = jnp.where(upper, high, low)
        send = jnp.where(upper, low, high)
        current = keep + xor_swap(send, axis, bit)
    for bit in reversed(order):
        upper = ((index >> bit) & 1) == 1
        other = xor_swap(current, axis, bit)
        current = jnp.where(
            upper, jnp.concatenate([other, current]), jnp.concatenate([current, other])
        )
    return current


def halve_stage(value, axis, bit, wire):
    half = value.shape[0] // 2
    upper = ((lax.axis_index(axis) >> bit) & 1) == 1
    low, high = value[:half], value[half:]
    keep = jnp.where(upper, high, low).astype(jnp.float32)
    send = jnp.where(upper, low, high)
    return keep + xor_swap(send.astype(wire), axis, bit).astype(jnp.float32)


def double_stage(value, axis, bit):
    upper = ((lax.axis_index(axis) >> bit) & 1) == 1
    other = xor_swap(value, axis, bit)
    return jnp.where(upper, jnp.concatenate([other, value]), jnp.concatenate([value, other]))


NEAR_BITS = (2, 4)


def grad_sum(partial):
    stream_count = lax.axis_size("stream")
    tm_count = lax.axis_size("tm")
    stream_bits = stream_count.bit_length() - 1
    tm_bits = tm_count.bit_length() - 1
    rows, grads = partial
    tokens, features = rows.shape
    if (
        stream_count != 1 << stream_bits
        or tm_count != 1 << tm_bits
        or stream_bits == 0
        or tm_bits == 0
        or features % (2 * stream_count)
        or grads.shape[1] % 256
    ):
        shard = lax.psum_scatter(
            contract_first(rows, grads).astype(jnp.bfloat16), "stream", scatter_dimension=0, tiled=True
        ).astype(jnp.float32)
        return lax.psum(shard, "tm")
    stream_index = lax.axis_index("stream")
    core = lax.axis_index("tm") % 2
    half_cols = grads.shape[1] // 2
    paired = rows.reshape(tokens, stream_count // 2, 2, features // stream_count)
    even = paired[:, :, 0].reshape(tokens, features // 2)
    odd = paired[:, :, 1].reshape(tokens, features // 2)
    upper = (stream_index & 1) == 1
    ordered = jnp.concatenate([jnp.where(upper, odd, even), jnp.where(upper, even, odd)], axis=1)
    mine_cols = lax.dynamic_slice_in_dim(grads, core * half_cols, half_cols, 1)
    other_cols = lax.dynamic_slice_in_dim(grads, (1 - core) * half_cols, half_cols, 1)
    current = contract_first(ordered, mine_cols) + xor_swap(
        contract_first(ordered, other_cols).astype(jnp.bfloat16), "tm", 0
    ).astype(jnp.float32)
    half_rows = features // 2
    current = current[:half_rows] + xor_swap(
        current[half_rows:].astype(jnp.bfloat16), "stream", 0
    ).astype(jnp.float32)
    for bit in reversed(range(1, stream_bits)):
        current = halve_stage(current, "stream", bit, jnp.bfloat16)
    near = [bit for bit in NEAR_BITS if bit < tm_bits]
    near = near[: max(0, current.shape[0].bit_length() - 1)]
    for bit in near:
        current = halve_stage(current, "tm", bit, jnp.bfloat16)
    for bit in range(1, tm_bits):
        if bit not in near:
            rounded = current.astype(jnp.bfloat16)
            current = rounded.astype(jnp.float32) + xor_swap(rounded, "tm", bit).astype(jnp.float32)
    for bit in reversed(near):
        current = double_stage(current, "tm", bit)
    other = xor_swap(current, "tm", 0)
    return jnp.where(
        core == 1,
        jnp.concatenate([other, current], axis=1),
        jnp.concatenate([current, other], axis=1),
    )


def ring_source(linear, shift, stream_count):
    tm_index, stream_index = divmod(linear, stream_count)
    ring = 2 * stream_count
    position = ((tm_index >> 1) & 1) * stream_count + stream_index
    moved = (position + shift) % ring
    tm_moved = (tm_index & ~2) | ((moved // stream_count) << 1)
    return tm_moved * stream_count + moved % stream_count


def ring_pull(value, shift):
    stream_count = lax.axis_size("stream")
    total = lax.axis_size("tm") * stream_count
    pairs = [(ring_source(target, shift, stream_count), target) for target in range(total)]
    return lax.ppermute(value, ("tm", "stream"), pairs)


def ring_gather(block):
    stream_count = lax.axis_size("stream")
    if stream_count != 4 or lax.axis_size("tm") % 4 or block.shape[1] % 256:
        return lax.all_gather(block, "stream", axis=0, tiled=True)
    rows, width = block.shape
    stream_index = lax.axis_index("stream")
    split = width // 2
    two_away = jnp.concatenate(
        [ring_pull(block[:, :split], 2), ring_pull(block[:, split:], -2)], axis=1
    )
    arrived = [block, ring_pull(block, 1), two_away, ring_pull(block, -1)]
    placed = []
    for position in range(stream_count):
        offset = (position - stream_index) % stream_count
        chosen = arrived[3]
        for slot in (2, 1, 0):
            chosen = jnp.where(offset == slot, arrived[slot], chosen)
        placed.append(chosen)
    return jnp.concatenate(placed, axis=0)


def ring_gather_both(block, core):
    stream_count = lax.axis_size("stream")
    stream_index = lax.axis_index("stream")
    split = block.shape[1] // 2
    two_away = jnp.concatenate(
        [ring_pull(block[:, :split], 2), ring_pull(block[:, split:], -2)], axis=1
    )
    arrived = [block, ring_pull(block, 1), two_away, ring_pull(block, -1)]
    partner = [xor_swap(piece, "tm", 0) for piece in arrived]
    halves = []
    for first in (True, False):
        pieces = [
            jnp.where((core == 0) == first, own, theirs) for own, theirs in zip(arrived, partner)
        ]
        placed = []
        for position in range(stream_count):
            offset = (position - stream_index) % stream_count
            chosen = pieces[3]
            for slot in (2, 1, 0):
                chosen = jnp.where(offset == slot, pieces[slot], chosen)
            placed.append(chosen)
        halves.append(jnp.concatenate(placed, axis=0))
    return jnp.concatenate(halves, axis=1)


def contract_last(left, right):
    return lax.dot_general(
        left, right, (((1,), (1,)), ((), ())), preferred_element_type=jnp.float32
    )


def contract_first(left, right):
    return lax.dot_general(
        left, right, (((0,), (0,)), ((), ())), preferred_element_type=jnp.float32
    )


def per_device(series, loss_grad, query_weight, keyval_weight, output_weight, lengths):
    record_rows = series[0]
    outer_grad = loss_grad[0]
    valid_count = lengths[0]
    shard_tokens = record_rows.shape[0]
    keyval_width = keyval_weight.shape[1]
    key_width = keyval_width // 2
    group_size = HEADS // KV_HEADS
    tile_rows = min(128, shard_tokens)
    key_span = REACH * shard_tokens + tile_rows
    score_scale = HEAD_DIM ** (-0.5)
    anchor = lax.axis_index("tm") * shard_tokens
    query_width = query_weight.shape[1]
    weights_local = jnp.concatenate([query_weight, keyval_weight, output_weight], axis=1)
    if lax.axis_size("tm") % 2 == 0 and weights_local.shape[1] % 256 == 0:
        half_width = weights_local.shape[1] // 2
        core = lax.axis_index("tm") % 2
        mine = lax.dynamic_slice_in_dim(weights_local, core * half_width, half_width, 1)
        if lax.axis_size("stream") == 4 and half_width % 256 == 0:
            weights_full = ring_gather_both(mine, core)
        else:
            mine = ring_gather(mine)
            other = xor_swap(mine, "tm", 0)
            weights_full = jnp.concatenate(
                [jnp.where(core == 0, mine, other), jnp.where(core == 0, other, mine)], axis=1
            )
    else:
        weights_full = lax.all_gather(weights_local, "stream", axis=0, tiled=True)
    query_full = weights_full[:, :query_width]
    keyval_full = weights_full[:, query_width : query_width + keyval_width]
    output_full = weights_full[:, query_width + keyval_width :]
    queries = jnp.dot(record_rows, query_full, preferred_element_type=jnp.float32).astype(
        jnp.bfloat16
    )
    keyvals = jnp.dot(record_rows, keyval_full, preferred_element_type=jnp.float32).astype(
        jnp.bfloat16
    )
    attn_grad = contract_last(outer_grad, output_full).astype(jnp.bfloat16)
    earlier = [shifted(keyvals, "tm", offset) for offset in range(REACH, 0, -1)]
    window_keyvals = jnp.concatenate(earlier + [keyvals], axis=0)
    query_block = queries[0:tile_rows].reshape(tile_rows, KV_HEADS, group_size, HEAD_DIM)
    key_block = window_keyvals[0:key_span, :key_width].reshape(key_span, KV_HEADS, HEAD_DIM)
    value_block = window_keyvals[0:key_span, key_width:].reshape(key_span, KV_HEADS, HEAD_DIM)
    query_pos = anchor + jnp.arange(tile_rows, dtype=jnp.int32)
    key_pos = anchor - REACH * shard_tokens + jnp.arange(key_span, dtype=jnp.int32)
    live_rows = query_pos < valid_count
    allowed = (key_pos[None, :] <= query_pos[:, None]) & (
        query_pos[:, None] - key_pos[None, :] < REACH * shard_tokens
    )
    allowed = (
        allowed
        & (key_pos[None, :] >= 0)
        & (key_pos[None, :] < valid_count)
        & live_rows[:, None]
    )
    scores = (
        jnp.einsum("qgjd,kgd->gjqk", query_block, key_block, preferred_element_type=jnp.float32)
        * score_scale
    )
    masked = jnp.where(allowed, scores, -1e30)
    row_max = jnp.max(masked, axis=-1, keepdims=True)
    terms = jnp.where(allowed, jnp.exp(masked - row_max), 0.0)
    denom = jnp.sum(terms, axis=-1, keepdims=True)
    denom = jnp.where(live_rows[:, None], denom, 1.0)
    attn_probs = (terms * (1.0 / denom)).astype(jnp.bfloat16)
    attn_block = jnp.einsum(
        "gjqk,kgd->qgjd", attn_probs, value_block, preferred_element_type=jnp.float32
    ).astype(jnp.bfloat16)
    grad_block = attn_grad[0:tile_rows].reshape(tile_rows, KV_HEADS, group_size, HEAD_DIM)
    row_delta = jnp.transpose(
        jnp.sum(grad_block.astype(jnp.float32) * attn_block.astype(jnp.float32), axis=-1),
        (1, 2, 0),
    )[..., None]
    prob_grad = jnp.einsum(
        "qgjd,kgd->gjqk", grad_block, value_block, preferred_element_type=jnp.float32
    )
    score_grad = (
        attn_probs.astype(jnp.float32) * (prob_grad - row_delta) * score_scale
    ).astype(jnp.bfloat16)
    query_grad_all = (
        jnp.einsum("gjqk,kgd->qgjd", score_grad, key_block, preferred_element_type=jnp.float32)
        .astype(jnp.bfloat16)
        .reshape(tile_rows, KV_HEADS * group_size * HEAD_DIM)
    )
    key_grad = jnp.einsum(
        "gjqk,qgjd->kgd", score_grad, query_block, preferred_element_type=jnp.float32
    ).reshape(key_span, key_width)
    value_grad = jnp.einsum(
        "gjqk,qgjd->kgd", attn_probs, grad_block, preferred_element_type=jnp.float32
    ).reshape(key_span, key_width)
    partial_value = jnp.concatenate([key_grad, value_grad], axis=1)

    def shard_slot(offset):
        return partial_value[(REACH - offset) * shard_tokens : (REACH - offset + 1) * shard_tokens]

    summed = shard_slot(0)
    for offset in range(1, REACH + 1):
        summed = summed + shifted(shard_slot(offset).astype(jnp.bfloat16), "tm", -offset).astype(
            jnp.float32
        )
    keyval_grads = summed.astype(jnp.bfloat16)
    input_grad = contract_last(query_grad_all, query_full) + contract_last(
        keyval_grads, keyval_full
    )
    input_grad = input_grad.astype(jnp.bfloat16)
    weight_grad = grad_sum((record_rows, keyval_grads))
    return (input_grad[None], weight_grad)


def solution(mesh):
    placed = (
        P("stream", "tm", None),
        P("stream", "tm", None),
        P("stream", None),
        P("stream", None),
        P("stream", None),
        P("stream"),
    )
    return jax.shard_map(
        per_device,
        mesh=mesh,
        in_specs=placed,
        out_specs=(P("stream", "tm", None), P("stream", None)),
        check_vma=False,
    )
```
